128 devices in a mesh: tile: 4 (over x), depth: 32 (over z, y, core).
Axes of the slice: x: 4, y: 4, z: 4, core: 2. Of those that a mesh axis runs over, the one named last changes fastest.
Arguments:
- prior_noise: float32 [4, 512, 64, 128], P(None, 'depth', 'tile'), may hold values from -6 to 6
- kappa_sq: float32 [512, 64, 128], P('depth', 'tile'), may hold values from 0.05 to 0.5
- horiz_cond: float32 [512, 64, 128], P('depth', 'tile'), may hold values from 0.3 to 1
- vert_cond: float32 [512, 64, 128], P('depth', 'tile'), may hold values from 0.8 to 2.5
- line_lower: float32 [512, 64, 128], P('depth', 'tile'), may hold values from -1 to -0.4, as said below
- line_pivot: float32 [512, 64, 128], P('depth', 'tile'), may hold values from 1 to 4
- deflation: float32 [16, 512, 64, 128], P(None, 'depth', 'tile'), may hold values from -1.1 to 1.1
- obs_value: float32 [4, 4, 32, 32, 16], P(None, 'tile', 'depth'), may hold values from -8 to 8
- obs_weight: float32 [4, 32, 32, 16], P('tile', 'depth'), may hold values from 1 to 8
- obs_cell: int32 [4, 32, 32, 16], P('tile', 'depth'), may hold values from 0 to 32767, as said below
- obs_count: int32 [4, 32, 32], P('tile', 'depth'), may hold values from 0 to 16, as said below
Outputs:
- solution: float32 [4, 512, 64, 128], P(None, 'depth', 'tile')
- residual: float32 [4, 512, 64, 128], P(None, 'depth', 'tile')
The draws below stay inside these ranges and needn't reach their ends.
Inputs may be any that keep to these rules, and one draw needn't show every extreme that they name: `obs_cell`: the number of a cell within the block of the destination's tile and depth index. `obs_count`: in every tile some destination depth index receives 16 observations from every source depth index. `line_lower`: every entry lies strictly above -1.
All inputs are finite; a program needn't handle non-finite values.
Results may differ from the reference program's by a relative error of at most 0.0003.
Values sent between devices are 32-bit elements; how exact they have to be, the bound alone decides.
No kernel may reach another device: no remote copies, remote signals or barrier semaphores. Data moves between devices by JAX's collectives and lax.ppermute only.
A program may use at most 128 MiB of HBM per device.

```python
import math
import jax
import jax.numpy as jnp
from jax import lax

CZ = 16
CX = 16
NY = 128
S = 4
NDEF = 16
ITERS = 2
CAP = 16
GRID_LAYERS = 512
NX = 64
N_TILE = 4
N_DEPTH = 32


def draw_line_lower(key, part):
    random_key_list = jax.random.split(key, 4)
    low_rate = math.log(1.0 / (2 * GRID_LAYERS))
    high_rate = math.log(1.0 / 16)
    rate_col = jnp.exp(jax.random.uniform(random_key_list[0], (1, NX, NY), jnp.float32, low_rate, high_rate))
    rough_part = jax.random.uniform(random_key_list[1], (GRID_LAYERS, NX, NY), jnp.float32, 0.5, 2.0)
    refresh_position = jax.random.uniform(random_key_list[2], (GRID_LAYERS, 1, 1), jnp.float32) < 3.0 / GRID_LAYERS
    refresh_length = jax.random.uniform(random_key_list[3], (GRID_LAYERS, 1, 1), jnp.float32, 0.5, 0.8)
    cholesky_factor = jnp.where(refresh_position, refresh_length, 1.0)
    return -(1.0 - rate_col * rough_part) * cholesky_factor


def draw_deflation(key, part):
    random_key_list = jax.random.split(key, 3)
    frequency = jax.random.randint(random_key_list[0], (NDEF, 3), 1, 4).astype(jnp.float32)
    phase_shift = jax.random.uniform(random_key_list[1], (NDEF, 3), jnp.float32, 0.0, math.pi)
    amount = 0.05
    jitter = jax.random.uniform(random_key_list[2], (NDEF, GRID_LAYERS, NX, NY), jnp.float32, -1.0, 1.0)
    along_z = (jnp.arange(GRID_LAYERS, dtype=jnp.float32) + 0.5) / GRID_LAYERS
    along_x = (jnp.arange(NX, dtype=jnp.float32) + 0.5) / NX
    along_y = (jnp.arange(NY, dtype=jnp.float32) + 0.5) / NY
    wave_z = jnp.sin(math.pi * frequency[:, 0:1] * along_z[None] + phase_shift[:, 0:1])
    wave_x = jnp.sin(math.pi * frequency[:, 1:2] * along_x[None] + phase_shift[:, 1:2])
    wave_y = jnp.sin(math.pi * frequency[:, 2:3] * along_y[None] + phase_shift[:, 2:3])
    result = wave_z[:, :, None, None] * wave_x[:, None, :, None] * wave_y[:, None, None, :]
    return result * (1.0 + amount * jitter)


def draw_obs_cell(key, part):
    cell_ids = jax.random.randint(key, (N_TILE, N_DEPTH, N_DEPTH, CAP), 0, CZ * CX * NY)
    cell_ids = cell_ids.at[0, 0, 0, 0].set(CZ * CX * NY - 1)
    return cell_ids.at[0, 0, 0, 1].set(0)


def draw_obs_count(key, part):
    random_key_list = jax.random.split(key, 2)
    counts_drawn = jax.random.randint(random_key_list[0], (N_TILE, N_DEPTH, N_DEPTH), 0, CAP + 1)
    complete_target = jax.random.randint(random_key_list[1], (N_TILE, 1, 1), 0, N_DEPTH)
    dest_index = lax.broadcasted_iota(jnp.int32, (N_TILE, N_DEPTH, N_DEPTH), 1)
    return jnp.where(dest_index == complete_target, CAP, counts_drawn)


def levels(rng, extent, cuts, smallest, high):
    factor_of, own = 1.0, jax.random.fold_in(rng, 6)
    for dim, blocks in cuts:
        steps = jnp.exp(jax.random.uniform(jax.random.fold_in(own, dim), (blocks,), jnp.float32, smallest / len(cuts), high / len(cuts)))
        factor_of = factor_of * jnp.repeat(steps, extent[dim] // blocks).reshape([-1 if axis == dim else 1 for axis in range(len(extent))])
    return factor_of


def noise(key, extent, spread, limit, cuts=(), kind=jnp.bfloat16):
    values = spread * jax.random.normal(key, extent, jnp.float32)
    if cuts:
        values = values * levels(key, extent, cuts, -0.22, 0.18)
    return jnp.clip(values, -limit, limit).astype(kind)


def setup_inputs(seed: int = 0) -> dict:
    splits = jax.random.split(jax.random.key(seed), 12)
    return {
        "prior_noise": noise(splits[0], (S, GRID_LAYERS, NX, NY), 1.0, 6.0, ((1, 32), (2, 4)), jnp.float32),
        "kappa_sq": jnp.clip(jnp.exp(math.log(0.5) - 2.3025851 * jax.random.uniform(splits[1], (GRID_LAYERS, NX, NY), jnp.float32) ** levels(splits[1], (GRID_LAYERS, NX, NY), ((0, 32), (1, 4)), -0.2, 0.2)), 0.05, 0.5),
        "horiz_cond": jnp.clip(jnp.exp(math.log(1.0) - 1.2039728 * jax.random.uniform(splits[2], (GRID_LAYERS, NX, NY), jnp.float32) ** levels(splits[2], (GRID_LAYERS, NX, NY), ((0, 32), (1, 4)), -0.2, 0.2)), 0.3, 1.0),
        "vert_cond": jnp.clip(jnp.exp(math.log(2.5) - 1.13943427 * jax.random.uniform(splits[3], (GRID_LAYERS, NX, NY), jnp.float32) ** levels(splits[3], (GRID_LAYERS, NX, NY), ((0, 32), (1, 4)), -0.2, 0.2)), 0.8, 2.5),
        "line_lower": draw_line_lower(jax.random.fold_in(splits[11], 71), 0),
        "line_pivot": jnp.clip(jnp.exp(math.log(4.0) - 1.3862944 * jax.random.uniform(splits[5], (GRID_LAYERS, NX, NY), jnp.float32) ** levels(splits[5], (GRID_LAYERS, NX, NY), ((0, 32), (1, 4)), -0.2, 0.2)), 1.0, 4.0),
        "deflation": draw_deflation(jax.random.fold_in(splits[11], 71), 0),
        "obs_value": noise(splits[7], (S, N_TILE, N_DEPTH, N_DEPTH, CAP), 1.5, 8.0, ((1, 4), (2, 32)), jnp.float32),
        "obs_weight": jnp.clip(jnp.exp(math.log(8.0) - 2.0794415 * jax.random.uniform(splits[8], (N_TILE, N_DEPTH, N_DEPTH, CAP), jnp.float32) ** levels(splits[8], (N_TILE, N_DEPTH, N_DEPTH, CAP), ((0, 4), (1, 32)), -0.2, 0.2)), 1.0, 8.0),
        "obs_cell": draw_obs_cell(jax.random.fold_in(splits[11], 71), 0),
        "obs_count": draw_obs_count(jax.random.fold_in(splits[11], 71), 0),
    }


PRECISE = lax.Precision.HIGHEST

def shifted(padded, d_layer, d_row, d_col):
    return padded[..., 1 + d_layer:1 + d_layer + GRID_LAYERS, 1 + d_row:1 + d_row + NX, 1 + d_col:1 + d_col + NY]

def stencil(vector_in, kappa_sq, horiz_cond, vert_cond):
    lead_dims = vector_in.ndim - 3
    padded = jnp.pad(vector_in, [(0, 0)] * lead_dims + [(1, 1)] * 3)
    horiz_pad = jnp.pad(horiz_cond, 1)
    vert_pad = jnp.pad(vert_cond, 1)
    horiz_sides = shifted(horiz_pad, 0, 1, 0) + shifted(horiz_pad, 0, -1, 0) + shifted(horiz_pad, 0, 0, 1) + shifted(horiz_pad, 0, 0, -1)
    vert_sides = shifted(vert_pad, 1, 0, 0) + shifted(vert_pad, -1, 0, 0)
    diag_part = kappa_sq + horiz_cond * horiz_sides + vert_cond * vert_sides
    flux_h = shifted(horiz_pad, 0, 1, 0) * shifted(padded, 0, 1, 0) + shifted(horiz_pad, 0, -1, 0) * shifted(padded, 0, -1, 0)
    flux_h = flux_h + shifted(horiz_pad, 0, 0, 1) * shifted(padded, 0, 0, 1) + shifted(horiz_pad, 0, 0, -1) * shifted(padded, 0, 0, -1)
    flux_v = shifted(vert_pad, 1, 0, 0) * shifted(padded, 1, 0, 0) + shifted(vert_pad, -1, 0, 0) * shifted(padded, -1, 0, 0)
    return diag_part * vector_in - horiz_cond * flux_h - vert_cond * flux_v

def line_solve(resid_in, line_lower, line_pivot):
    by_layer = jnp.moveaxis(resid_in, 1, 0)
    zero_carry = jnp.zeros(by_layer.shape[1:], by_layer.dtype)

    def recur(carried, element):
        result = element[0] - element[1] * carried
        return (result, result)
    final_down, forward = lax.scan(recur, zero_carry, (by_layer, line_lower))
    scaled = forward / line_pivot[:, None]
    upper_coef = jnp.concatenate([line_lower[1:], jnp.zeros_like(line_lower[:1])], 0)
    final_up, backward = lax.scan(recur, zero_carry, (scaled, upper_coef), reverse=True)
    return jnp.moveaxis(backward, 0, 1)

def observed(obs_value, obs_weight, obs_cell, obs_count):
    slot_index = lax.broadcasted_iota(jnp.int32, obs_cell.shape, 3)
    live_slot = (slot_index < obs_count[..., None]).astype(jnp.float32)
    weights = jnp.transpose(obs_weight, (0, 2, 1, 3)) * live_slot
    values = jnp.transpose(obs_value, (0, 1, 3, 2, 4))
    tile_at = lax.broadcasted_iota(jnp.int32, obs_cell.shape, 0)
    depth_at = lax.broadcasted_iota(jnp.int32, obs_cell.shape, 1)
    layer_at = depth_at * CZ + obs_cell // (CX * NY)
    row_at = tile_at * CX + obs_cell // NY % CX
    column = obs_cell % NY
    target = ((layer_at * NX + row_at) * NY + column).reshape(-1)
    diag_obs = jnp.zeros((GRID_LAYERS * NX * NY,), jnp.float32).at[target].add(weights.reshape(-1))
    rhs_obs = jnp.zeros((S, GRID_LAYERS * NX * NY), jnp.float32).at[:, target].add((values * weights[None]).reshape(S, -1))
    return (diag_obs.reshape(GRID_LAYERS, NX, NY), rhs_obs.reshape(S, GRID_LAYERS, NX, NY))

def reference(prior_noise, kappa_sq, horiz_cond, vert_cond, line_lower, line_pivot, deflation, obs_value, obs_weight, obs_cell, obs_count):
    obs_diag, obs_rhs = observed(obs_value, obs_weight, obs_cell, obs_count)

    def kapply(vector_in):
        return stencil(vector_in, kappa_sq, horiz_cond, vert_cond)

    def aapply(vector_in):
        return kapply(kapply(vector_in)) + obs_diag * vector_in
    right_side = kapply(prior_noise) + obs_rhs
    basis_flat = deflation.reshape(NDEF, -1)

    def gram_row(vector_in):
        return jnp.dot(basis_flat, aapply(vector_in).reshape(-1), precision=PRECISE)
    gram_matrix = lax.map(gram_row, deflation)
    gram_matrix = 0.5 * (gram_matrix + gram_matrix.T)
    chol_factor = jnp.linalg.cholesky(gram_matrix)

    def coarse(terms):
        return jax.scipy.linalg.cho_solve((chol_factor, True), terms)

    def expand(coarse_coef):
        return jnp.dot(coarse_coef.T, basis_flat, precision=PRECISE).reshape(S, GRID_LAYERS, NX, NY)

    def project(vectors):
        return jnp.dot(basis_flat, vectors.reshape(S, -1).T, precision=PRECISE)

    def inner_sum(left_side, right_part):
        return jnp.sum(left_side * right_part, axis=(1, 2, 3))
    coarse_coef = coarse(project(right_side))
    solution = expand(coarse_coef)
    residual = right_side - aapply(solution)
    precond = line_solve(residual, line_lower, line_pivot)
    rz_now = inner_sum(residual, precond)
    coarse_dir = coarse(project(aapply(precond)))
    direction = precond - expand(coarse_dir)
    for iteration in range(ITERS):
        image_dir = aapply(direction)
        step_field = (rz_now / inner_sum(direction, image_dir))[:, None, None, None]
        solution = solution + step_field * direction
        residual = residual - step_field * image_dir
        if iteration + 1 < ITERS:
            precond = line_solve(residual, line_lower, line_pivot)
            rz_next = inner_sum(residual, precond)
            coarse_dir = coarse(project(aapply(precond)))
            beta_ratio = (rz_next / rz_now)[:, None, None, None]
            direction = precond + beta_ratio * direction - expand(coarse_dir)
            rz_now = rz_next
    return (solution, residual)
```

```python
import jax
import jax.numpy as jnp
from jax import lax
from jax.experimental import pallas as pl
from jax.sharding import PartitionSpec as P

ITERS = 2


PRECISE = lax.Precision.HIGHEST


def xor_round(x, axis, masks):
    count = lax.axis_size(axis)
    parts = [lax.ppermute(x, axis, [(i, i ^ m) for i in range(count)]) for m in masks]
    for part in parts:
        x = x + part
    return x


def all_sum(x):
    x = xor_round(x, "tile", tuple(range(1, lax.axis_size("tile"))))
    count, span = lax.axis_size("depth"), 1
    while span < count:
        radix = 4 if count // span >= 4 else 2
        x = xor_round(x, "depth", tuple(span * j for j in range(1, radix)))
        span *= radix
    return x


def neighbours(array, axis, dim):
    count, length = lax.axis_size(axis), array.shape[dim]
    up = [(i, i + 1) for i in range(count - 1)]
    down = [(i + 1, i) for i in range(count - 1)]
    last = lax.slice_in_dim(array, length - 1, length, axis=dim)
    first = lax.slice_in_dim(array, 0, 1, axis=dim)
    before = lax.ppermute(last, axis, up)
    after = lax.ppermute(first, axis, down)
    lower = jnp.concatenate([before, lax.slice_in_dim(array, 0, length - 1, axis=dim)], dim)
    upper = jnp.concatenate([lax.slice_in_dim(array, 1, length, axis=dim), after], dim)
    return lower, upper


def column_up(vector_in):
    return jnp.concatenate([vector_in[..., 1:], jnp.zeros_like(vector_in[..., :1])], -1)


def column_down(vector_in):
    return jnp.concatenate([jnp.zeros_like(vector_in[..., :1]), vector_in[..., :-1]], -1)


def cells_dot(left_rows, right_rows):
    return lax.dot_general(left_rows, right_rows, (((1,), (1,)), ((), ())), precision=PRECISE)


def prep_kernel(low_ref, piv_ref, gd_ref, gu_ref, h_ref, c_ref):
    layers = low_ref.shape[0]
    g = -low_ref[0]
    gd_ref[0] = g
    for i in range(1, layers):
        g = -low_ref[i] * g
        gd_ref[i] = g
    u = jnp.ones_like(g)
    gu_ref[layers - 1] = u
    for i in range(layers - 2, -1, -1):
        u = -low_ref[i + 1] * u
        gu_ref[i] = u
    z = gd_ref[layers - 1] / piv_ref[layers - 1]
    h_ref[layers - 1] = z
    for i in range(layers - 2, -1, -1):
        z = gd_ref[i] / piv_ref[i] - low_ref[i + 1] * z
        h_ref[i] = z
    c_ref[0] = gd_ref[layers - 1]
    c_ref[1] = -low_ref[0] * z
    c_ref[2] = -low_ref[0] * u


def sweep_kernel(r_ref, low_ref, piv_ref, bw_ref, msg_ref):
    layers = r_ref.shape[1]
    y = r_ref[:, 0]
    bw_ref[:, 0] = y / piv_ref[0][None]
    for i in range(1, layers):
        y = r_ref[:, i] - low_ref[i][None] * y
        bw_ref[:, i] = y / piv_ref[i][None]
    msg_ref[0] = y
    z = bw_ref[:, layers - 1]
    for i in range(layers - 2, -1, -1):
        z = bw_ref[:, i] - low_ref[i + 1][None] * z
        bw_ref[:, i] = z
    msg_ref[1] = -low_ref[0][None] * z


def scan_kernel(msg_ref, c_ref, e_ref, t_ref):
    count = msg_ref.shape[0]
    e = jnp.zeros(msg_ref.shape[2:], jnp.float32)
    e_ref[0] = e
    for k in range(count - 1):
        e = msg_ref[k, 0] + c_ref[k, 0][None] * e
        e_ref[k + 1] = e
    t = jnp.zeros_like(e)
    t_ref[count - 1] = t
    for k in range(count - 1, 0, -1):
        offset = msg_ref[k, 1] + c_ref[k, 1][None] * e_ref[k]
        t = offset + c_ref[k, 2][None] * t
        t_ref[k - 1] = t


def per_device(
    prior_noise,
    kappa_sq,
    horiz_cond,
    vert_cond,
    line_lower,
    line_pivot,
    deflation,
    obs_value,
    obs_weight,
    obs_cell,
    obs_count,
):
    samples = prior_noise.shape[0]
    vectors = deflation.shape[0]
    block_shape = prior_noise.shape[1:]
    layers = block_shape[0]
    cell_count = kappa_sq.size
    f32 = jnp.float32
    got_value, got_weight = (
        lax.all_to_all(obs_value, "depth", split_axis=3, concat_axis=2, tiled=True),
        lax.all_to_all(obs_weight[None], "depth", split_axis=3, concat_axis=2, tiled=True),
    )
    slot_index = lax.broadcasted_iota(jnp.int32, obs_cell.shape[2:], 1)
    live_slot = (slot_index < obs_count[0, 0][:, None]).astype(f32).reshape(-1)
    weights = got_weight.reshape(-1) * live_slot
    targets = obs_cell.reshape(-1)
    obs_diag = jnp.zeros((cell_count,), f32).at[targets].add(weights).reshape(block_shape)
    obs_rhs = (
        jnp.zeros((samples, cell_count), f32)
        .at[:, targets]
        .add(got_value.reshape(samples, -1) * weights[None])
    )
    obs_rhs = obs_rhs.reshape(prior_noise.shape)

    coefs = jnp.stack([horiz_cond, vert_cond])
    v_below, v_above = neighbours(coefs[1:], "depth", 1)
    h_rowm, h_rowp = neighbours(coefs[:1], "tile", 2)
    v_below, v_above, h_rowm, h_rowp = v_below[0], v_above[0], h_rowm[0], h_rowp[0]
    h_colp, h_colm = column_up(horiz_cond), column_down(horiz_cond)
    diag_part = (
        kappa_sq
        + horiz_cond * (h_rowp + h_rowm + h_colp + h_colm)
        + vert_cond * (v_above + v_below)
    )
    c_below, c_above = vert_cond * v_below, vert_cond * v_above
    c_rowm, c_rowp = horiz_cond * h_rowm, horiz_cond * h_rowp
    c_colm, c_colp = horiz_cond * h_colm, horiz_cond * h_colp

    def kapply(u):
        below, above = neighbours(u, "depth", 1)
        rowm, rowp = neighbours(u, "tile", 2)
        flux = (
            c_rowp * rowp
            + c_rowm * rowm
            + c_colp * column_up(u)
            + c_colm * column_down(u)
            + c_above * above
            + c_below * below
        )
        return diag_part * u - flux

    field = jax.ShapeDtypeStruct(block_shape, f32)
    gain_down, gain_up, h_field, consts = pl.pallas_call(
        prep_kernel,
        out_shape=(field, field, field, jax.ShapeDtypeStruct((3,) + block_shape[1:], f32)),
    )(line_lower, line_pivot)
    consts_all = lax.all_gather(consts, "depth")

    def line_solve(resid_in):
        back, message = pl.pallas_call(
            sweep_kernel,
            out_shape=(
                jax.ShapeDtypeStruct(resid_in.shape, f32),
                jax.ShapeDtypeStruct((2, samples) + block_shape[1:], f32),
            ),
        )(resid_in, line_lower, line_pivot)
        messages = lax.all_gather(message, "depth")
        count = messages.shape[0]
        enter_all, top_all = pl.pallas_call(
            scan_kernel,
            out_shape=(
                jax.ShapeDtypeStruct((count, samples) + block_shape[1:], f32),
                jax.ShapeDtypeStruct((count, samples) + block_shape[1:], f32),
            ),
        )(messages, consts_all)
        mine = lax.axis_index("depth")
        enter = lax.dynamic_index_in_dim(enter_all, mine, 0, keepdims=False)
        top = lax.dynamic_index_in_dim(top_all, mine, 0, keepdims=False)
        return back + enter[:, None] * h_field[None] + top[:, None] * gain_up[None]

    right_side = kapply(prior_noise) + obs_rhs
    basis_flat = deflation.reshape(vectors, cell_count)
    kbasis = kapply(deflation)
    abasis_flat = (kapply(kbasis) + obs_diag * deflation).reshape(vectors, cell_count)
    gram_part = cells_dot(basis_flat, abasis_flat)
    proj_part = cells_dot(basis_flat, right_side.reshape(samples, cell_count))
    first = all_sum(jnp.concatenate([gram_part.reshape(-1), proj_part.reshape(-1)]))
    gram_total = first[: vectors * vectors].reshape(vectors, vectors)
    proj_rhs = first[vectors * vectors :].reshape(vectors, samples)
    gram_matrix = 0.5 * (gram_total + gram_total.T)
    chol_factor = jnp.linalg.cholesky(gram_matrix)

    def coarse(terms):
        return jax.scipy.linalg.cho_solve((chol_factor, True), terms)

    def expand(rows_flat, coarse_coef):
        return jnp.dot(coarse_coef.T, rows_flat, precision=PRECISE).reshape(prior_noise.shape)

    def inner_sum(left_side, right_part):
        return jnp.sum(left_side * right_part, axis=(1, 2, 3))

    def project(field_in):
        return cells_dot(abasis_flat, field_in.reshape(samples, cell_count))

    coarse_coef = coarse(proj_rhs)
    solution = expand(basis_flat, coarse_coef)
    residual = right_side - expand(abasis_flat, coarse_coef)

    precond = line_solve(residual)
    k_precond = kapply(precond)
    sums = all_sum(
        jnp.concatenate(
            [
                inner_sum(residual, precond),
                inner_sum(k_precond, k_precond) + inner_sum(obs_diag * precond, precond),
                project(precond).reshape(-1),
            ]
        )
    )
    rz_now, pap = sums[:samples], sums[samples : 2 * samples]
    proj_now = sums[2 * samples :].reshape(vectors, samples)
    a_precond = kapply(k_precond) + obs_diag * precond
    coarse_dir = coarse(proj_now)
    direction = precond - expand(basis_flat, coarse_dir)
    image_dir = a_precond - expand(abasis_flat, coarse_dir)
    curve_val = pap - jnp.sum(coarse_dir * proj_now, 0)
    step_field = (rz_now / curve_val)[:, None, None, None]
    solution = solution + step_field * direction
    residual = residual - step_field * image_dir

    precond = line_solve(residual)
    k_precond = kapply(precond)
    sums = all_sum(
        jnp.concatenate(
            [
                inner_sum(residual, precond),
                inner_sum(k_precond, k_precond) + inner_sum(obs_diag * precond, precond),
                inner_sum(image_dir, precond),
                project(precond).reshape(-1),
                project(direction).reshape(-1),
            ]
        )
    )
    rz_next, pap, cross = sums[:samples], sums[samples : 2 * samples], sums[2 * samples : 3 * samples]
    rest = sums[3 * samples :]
    proj_now = rest[: vectors * samples].reshape(vectors, samples)
    proj_old = rest[vectors * samples :].reshape(vectors, samples)
    a_precond = kapply(k_precond) + obs_diag * precond
    coarse_dir = coarse(proj_now)
    beta = rz_next / rz_now
    beta_ratio = beta[:, None, None, None]
    direction = precond + beta_ratio * direction - expand(basis_flat, coarse_dir)
    image_dir = a_precond + beta_ratio * image_dir - expand(abasis_flat, coarse_dir)
    curve_val = (
        pap
        + 2.0 * beta * cross
        + beta * beta * curve_val
        - jnp.sum(coarse_dir * proj_now, 0)
        - 2.0 * beta * jnp.sum(coarse_dir * proj_old, 0)
    )
    step_field = (rz_next / curve_val)[:, None, None, None]
    solution = solution + step_field * direction
    residual = residual - step_field * image_dir
    return (solution, residual)


def solution(mesh):
    return jax.shard_map(
        per_device,
        mesh=mesh,
        in_specs=(
            P(None, "depth", "tile", None),
            P("depth", "tile", None),
            P("depth", "tile", None),
            P("depth", "tile", None),
            P("depth", "tile", None),
            P("depth", "tile", None),
            P(None, "depth", "tile", None),
            P(None, "tile", "depth", None, None),
            P("tile", "depth", None, None),
            P("tile", "depth", None, None),
            P("tile", "depth", None),
        ),
        out_specs=(P(None, "depth", "tile", None), P(None, "depth", "tile", None)),
        check_vma=False,
    )
```

```python
import jax
import jax.numpy as jnp
from jax import lax
from jax.experimental import pallas as pl
from jax.sharding import PartitionSpec as P

ITERS = 2


PRECISE = lax.Precision.HIGHEST


def xor_round(x, axis, masks):
    count = lax.axis_size(axis)
    parts = [lax.ppermute(x, axis, [(i, i ^ m) for i in range(count)]) for m in masks]
    for part in parts:
        x = x + part
    return x


def all_sum(x):
    x = xor_round(x, "tile", tuple(range(1, lax.axis_size("tile"))))
    count, span = lax.axis_size("depth"), 1
    while span < count:
        radix = 4 if count // span >= 4 else 2
        x = xor_round(x, "depth", tuple(span * j for j in range(1, radix)))
        span *= radix
    return x


def neighbours(array, axis, dim):
    count, length = lax.axis_size(axis), array.shape[dim]
    up = [(i, i + 1) for i in range(count - 1)]
    down = [(i + 1, i) for i in range(count - 1)]
    last = lax.slice_in_dim(array, length - 1, length, axis=dim)
    first = lax.slice_in_dim(array, 0, 1, axis=dim)
    before = lax.ppermute(last, axis, up)
    after = lax.ppermute(first, axis, down)
    lower = jnp.concatenate([before, lax.slice_in_dim(array, 0, length - 1, axis=dim)], dim)
    upper = jnp.concatenate([lax.slice_in_dim(array, 1, length, axis=dim), after], dim)
    return lower, upper


def column_up(vector_in):
    return jnp.concatenate([vector_in[..., 1:], jnp.zeros_like(vector_in[..., :1])], -1)


def column_down(vector_in):
    return jnp.concatenate([jnp.zeros_like(vector_in[..., :1]), vector_in[..., :-1]], -1)


def cells_dot(left_rows, right_rows):
    return lax.dot_general(left_rows, right_rows, (((1,), (1,)), ((), ())), precision=PRECISE)


def prep_kernel(low_ref, piv_ref, gd_ref, gu_ref, h_ref, c_ref):
    layers = low_ref.shape[0]
    g = -low_ref[0]
    gd_ref[0] = g
    for i in range(1, layers):
        g = -low_ref[i] * g
        gd_ref[i] = g
    u = jnp.ones_like(g)
    gu_ref[layers - 1] = u
    for i in range(layers - 2, -1, -1):
        u = -low_ref[i + 1] * u
        gu_ref[i] = u
    z = gd_ref[layers - 1] / piv_ref[layers - 1]
    h_ref[layers - 1] = z
    for i in range(layers - 2, -1, -1):
        z = gd_ref[i] / piv_ref[i] - low_ref[i + 1] * z
        h_ref[i] = z
    c_ref[0] = gd_ref[layers - 1]
    c_ref[1] = -low_ref[0] * z
    c_ref[2] = -low_ref[0] * u


def sweep_kernel(r_ref, low_ref, piv_ref, bw_ref, msg_ref):
    layers = r_ref.shape[1]
    y = r_ref[:, 0]
    bw_ref[:, 0] = y / piv_ref[0][None]
    for i in range(1, layers):
        y = r_ref[:, i] - low_ref[i][None] * y
        bw_ref[:, i] = y / piv_ref[i][None]
    msg_ref[0] = y
    z = bw_ref[:, layers - 1]
    for i in range(layers - 2, -1, -1):
        z = bw_ref[:, i] - low_ref[i + 1][None] * z
        bw_ref[:, i] = z
    msg_ref[1] = -low_ref[0][None] * z


def scan_kernel(msg_ref, c_ref, e_ref, t_ref):
    count, samples = msg_ref.shape[0], e_ref.shape[1]
    base = 2 * samples
    e = jnp.zeros(e_ref.shape[1:], jnp.float32)
    e_ref[0] = e
    for k in range(count - 1):
        e = msg_ref[k, 0:samples] + c_ref[k, base][None] * e
        e_ref[k + 1] = e
    t = jnp.zeros_like(e)
    t_ref[count - 1] = t
    for k in range(count - 1, 0, -1):
        offset = msg_ref[k, samples:base] + c_ref[k, base + 1][None] * e_ref[k]
        t = offset + c_ref[k, base + 2][None] * t
        t_ref[k - 1] = t


def per_device(
    prior_noise,
    kappa_sq,
    horiz_cond,
    vert_cond,
    line_lower,
    line_pivot,
    deflation,
    obs_value,
    obs_weight,
    obs_cell,
    obs_count,
):
    samples = prior_noise.shape[0]
    vectors = deflation.shape[0]
    block_shape = prior_noise.shape[1:]
    layers = block_shape[0]
    cell_count = kappa_sq.size
    f32 = jnp.float32
    rows_per, cols = block_shape[1] * block_shape[0], block_shape[2]
    sent = jnp.concatenate([obs_value, obs_weight[None]], 0)
    got = lax.all_to_all(sent, "depth", split_axis=3, concat_axis=2, tiled=True)
    got_value, got_weight = got[:samples], got[samples]
    slot_index = lax.broadcasted_iota(jnp.int32, obs_cell.shape[2:], 1)
    live_slot = (slot_index < obs_count[0, 0][:, None]).astype(f32).reshape(-1)
    weights = got_weight.reshape(-1) * live_slot
    targets = obs_cell.reshape(-1)
    at_row, at_col = targets // cols, targets % cols
    obs_diag = jnp.zeros((rows_per, cols), f32).at[at_row, at_col].add(weights).reshape(block_shape)
    obs_rhs = (
        jnp.zeros((samples, rows_per, cols), f32)
        .at[:, at_row, at_col]
        .add(got_value.reshape(samples, -1) * weights[None])
    )
    obs_rhs = obs_rhs.reshape(prior_noise.shape)

    joint = jnp.concatenate(
        [prior_noise, deflation, horiz_cond[None], vert_cond[None]], 0
    )
    j_below, j_above = neighbours(joint, "depth", 1)
    j_rowm, j_rowp = neighbours(joint, "tile", 2)
    lead = samples + vectors
    v_below, v_above = j_below[lead + 1], j_above[lead + 1]
    h_rowm, h_rowp = j_rowm[lead], j_rowp[lead]
    h_colp, h_colm = column_up(horiz_cond), column_down(horiz_cond)
    diag_part = (
        kappa_sq
        + horiz_cond * (h_rowp + h_rowm + h_colp + h_colm)
        + vert_cond * (v_above + v_below)
    )
    c_below, c_above = vert_cond * v_below, vert_cond * v_above
    c_rowm, c_rowp = horiz_cond * h_rowm, horiz_cond * h_rowp
    c_colm, c_colp = horiz_cond * h_colm, horiz_cond * h_colp

    def kcombine(u, below, above, rowm, rowp):
        flux = (
            c_rowp * rowp
            + c_rowm * rowm
            + c_colp * column_up(u)
            + c_colm * column_down(u)
            + c_above * above
            + c_below * below
        )
        return diag_part * u - flux

    def kapply(u):
        below, above = neighbours(u, "depth", 1)
        rowm, rowp = neighbours(u, "tile", 2)
        return kcombine(u, below, above, rowm, rowp)

    field = jax.ShapeDtypeStruct(block_shape, f32)
    gain_down, gain_up, h_field, consts = pl.pallas_call(
        prep_kernel,
        out_shape=(field, field, field, jax.ShapeDtypeStruct((3,) + block_shape[1:], f32)),
    )(line_lower, line_pivot)
    width = 2 * samples

    def line_solve(resid_in, consts_all=None):
        back, message = pl.pallas_call(
            sweep_kernel,
            out_shape=(
                jax.ShapeDtypeStruct(resid_in.shape, f32),
                jax.ShapeDtypeStruct((2, samples) + block_shape[1:], f32),
            ),
        )(resid_in, line_lower, line_pivot)
        message = message.reshape((width,) + block_shape[1:])
        if consts_all is None:
            messages = lax.all_gather(jnp.concatenate([message, consts], 0), "depth")
            consts_all = messages
        else:
            messages = lax.all_gather(message, "depth")
        count = messages.shape[0]
        enter_all, top_all = pl.pallas_call(
            scan_kernel,
            out_shape=(
                jax.ShapeDtypeStruct((count, samples) + block_shape[1:], f32),
                jax.ShapeDtypeStruct((count, samples) + block_shape[1:], f32),
            ),
        )(messages, consts_all)
        mine = lax.axis_index("depth")
        enter = lax.dynamic_index_in_dim(enter_all, mine, 0, keepdims=False)
        top = lax.dynamic_index_in_dim(top_all, mine, 0, keepdims=False)
        result = back + enter[:, None] * h_field[None] + top[:, None] * gain_up[None]
        return result, consts_all

    k_joint = kcombine(
        joint[:lead], j_below[:lead], j_above[:lead], j_rowm[:lead], j_rowp[:lead]
    )
    right_side = k_joint[:samples] + obs_rhs
    basis_flat = deflation.reshape(vectors, cell_count)
    kbasis = k_joint[samples:]
    abasis_flat = (kapply(kbasis) + obs_diag * deflation).reshape(vectors, cell_count)
    gram_part = cells_dot(basis_flat, abasis_flat)
    proj_part = cells_dot(basis_flat, right_side.reshape(samples, cell_count))
    first = all_sum(jnp.concatenate([gram_part.reshape(-1), proj_part.reshape(-1)]))
    gram_total = first[: vectors * vectors].reshape(vectors, vectors)
    proj_rhs = first[vectors * vectors :].reshape(vectors, samples)
    gram_matrix = 0.5 * (gram_total + gram_total.T)
    chol_factor = jnp.linalg.cholesky(gram_matrix)

    def coarse(terms):
        return jax.scipy.linalg.cho_solve((chol_factor, True), terms)

    def expand(rows_flat, coarse_coef):
        return jnp.dot(coarse_coef.T, rows_flat, precision=PRECISE).reshape(prior_noise.shape)

    def inner_sum(left_side, right_part):
        return jnp.sum(left_side * right_part, axis=(1, 2, 3))

    def project(field_in):
        return cells_dot(abasis_flat, field_in.reshape(samples, cell_count))

    coarse_coef = coarse(proj_rhs)
    solution = expand(basis_flat, coarse_coef)
    residual = right_side - expand(abasis_flat, coarse_coef)

    precond, consts_all = line_solve(residual)
    k_precond = kapply(precond)
    sums = all_sum(
        jnp.concatenate(
            [
                inner_sum(residual, precond),
                inner_sum(k_precond, k_precond) + inner_sum(obs_diag * precond, precond),
                project(precond).reshape(-1),
            ]
        )
    )
    rz_now, pap = sums[:samples], sums[samples : 2 * samples]
    proj_now = sums[2 * samples :].reshape(vectors, samples)
    a_precond = kapply(k_precond) + obs_diag * precond
    coarse_dir = coarse(proj_now)
    direction = precond - expand(basis_flat, coarse_dir)
    image_dir = a_precond - expand(abasis_flat, coarse_dir)
    curve_val = pap - jnp.sum(coarse_dir * proj_now, 0)
    step_field = (rz_now / curve_val)[:, None, None, None]
    solution = solution + step_field * direction
    residual = residual - step_field * image_dir

    precond, _ = line_solve(residual, consts_all)
    k_precond = kapply(precond)
    sums = all_sum(
        jnp.concatenate(
            [
                inner_sum(residual, precond),
                inner_sum(k_precond, k_precond) + inner_sum(obs_diag * precond, precond),
                inner_sum(image_dir, precond),
                project(precond).reshape(-1),
                project(direction).reshape(-1),
            ]
        )
    )
    rz_next, pap, cross = sums[:samples], sums[samples : 2 * samples], sums[2 * samples : 3 * samples]
    rest = sums[3 * samples :]
    proj_now = rest[: vectors * samples].reshape(vectors, samples)
    proj_old = rest[vectors * samples :].reshape(vectors, samples)
    a_precond = kapply(k_precond) + obs_diag * precond
    coarse_dir = coarse(proj_now)
    beta = rz_next / rz_now
    beta_ratio = beta[:, None, None, None]
    direction = precond + beta_ratio * direction - expand(basis_flat, coarse_dir)
    image_dir = a_precond + beta_ratio * image_dir - expand(abasis_flat, coarse_dir)
    curve_val = (
        pap
        + 2.0 * beta * cross
        + beta * beta * curve_val
        - jnp.sum(coarse_dir * proj_now, 0)
        - 2.0 * beta * jnp.sum(coarse_dir * proj_old, 0)
    )
    step_field = (rz_next / curve_val)[:, None, None, None]
    solution = solution + step_field * direction
    residual = residual - step_field * image_dir
    return (solution, residual)


def solution(mesh):
    return jax.shard_map(
        per_device,
        mesh=mesh,
        in_specs=(
            P(None, "depth", "tile", None),
            P("depth", "tile", None),
            P("depth", "tile", None),
            P("depth", "tile", None),
            P("depth", "tile", None),
            P("depth", "tile", None),
            P(None, "depth", "tile", None),
            P(None, "tile", "depth", None, None),
            P("tile", "depth", None, None),
            P("tile", "depth", None, None),
            P("tile", "depth", None),
        ),
        out_specs=(P(None, "depth", "tile", None), P(None, "depth", "tile", None)),
        check_vma=False,
    )
```

```python
import jax
import jax.numpy as jnp
from jax import lax
from jax.experimental import pallas as pl
from jax.sharding import PartitionSpec as P

ITERS = 2


PRECISE = lax.Precision.HIGHEST


def xor_round(x, axis, masks):
    count = lax.axis_size(axis)
    parts = [lax.ppermute(x, axis, [(i, i ^ m) for i in range(count)]) for m in masks]
    for part in parts:
        x = x + part
    return x


def all_sum(x):
    x = xor_round(x, "tile", tuple(range(1, lax.axis_size("tile"))))
    count, span = lax.axis_size("depth"), 1
    while span < count:
        radix = 4 if count // span >= 4 else 2
        x = xor_round(x, "depth", tuple(span * j for j in range(1, radix)))
        span *= radix
    return x


def gather_depth(x):
    count = lax.axis_size("depth")
    spread = jnp.broadcast_to(x[None], (count,) + x.shape)
    return lax.all_to_all(spread, "depth", 0, 0, tiled=False)


def neighbours(array, axis, dim):
    count, length = lax.axis_size(axis), array.shape[dim]
    up = [(i, i + 1) for i in range(count - 1)]
    down = [(i + 1, i) for i in range(count - 1)]
    last = lax.slice_in_dim(array, length - 1, length, axis=dim)
    first = lax.slice_in_dim(array, 0, 1, axis=dim)
    before = lax.ppermute(last, axis, up)
    after = lax.ppermute(first, axis, down)
    lower = jnp.concatenate([before, lax.slice_in_dim(array, 0, length - 1, axis=dim)], dim)
    upper = jnp.concatenate([lax.slice_in_dim(array, 1, length, axis=dim), after], dim)
    return lower, upper


def column_up(vector_in):
    return jnp.concatenate([vector_in[..., 1:], jnp.zeros_like(vector_in[..., :1])], -1)


def column_down(vector_in):
    return jnp.concatenate([jnp.zeros_like(vector_in[..., :1]), vector_in[..., :-1]], -1)


def cells_dot(left_rows, right_rows):
    return lax.dot_general(left_rows, right_rows, (((1,), (1,)), ((), ())), precision=PRECISE)


def prep_kernel(low_ref, piv_ref, gd_ref, gu_ref, h_ref, c_ref):
    layers = low_ref.shape[0]
    g = -low_ref[0]
    gd_ref[0] = g
    for i in range(1, layers):
        g = -low_ref[i] * g
        gd_ref[i] = g
    u = jnp.ones_like(g)
    gu_ref[layers - 1] = u
    for i in range(layers - 2, -1, -1):
        u = -low_ref[i + 1] * u
        gu_ref[i] = u
    z = gd_ref[layers - 1] / piv_ref[layers - 1]
    h_ref[layers - 1] = z
    for i in range(layers - 2, -1, -1):
        z = gd_ref[i] / piv_ref[i] - low_ref[i + 1] * z
        h_ref[i] = z
    c_ref[0] = gd_ref[layers - 1]
    c_ref[1] = -low_ref[0] * z
    c_ref[2] = -low_ref[0] * u


def sweep_kernel(r_ref, low_ref, piv_ref, bw_ref, msg_ref):
    layers = r_ref.shape[1]
    y = r_ref[:, 0]
    bw_ref[:, 0] = y / piv_ref[0][None]
    for i in range(1, layers):
        y = r_ref[:, i] - low_ref[i][None] * y
        bw_ref[:, i] = y / piv_ref[i][None]
    msg_ref[0] = y
    z = bw_ref[:, layers - 1]
    for i in range(layers - 2, -1, -1):
        z = bw_ref[:, i] - low_ref[i + 1][None] * z
        bw_ref[:, i] = z
    msg_ref[1] = -low_ref[0][None] * z


def scan_kernel(msg_ref, c_ref, e_ref, t_ref):
    count, samples = msg_ref.shape[0], e_ref.shape[1]
    base = 2 * samples
    e = jnp.zeros(e_ref.shape[1:], jnp.float32)
    e_ref[0] = e
    for k in range(count - 1):
        e = msg_ref[k, 0:samples] + c_ref[k, base][None] * e
        e_ref[k + 1] = e
    t = jnp.zeros_like(e)
    t_ref[count - 1] = t
    for k in range(count - 1, 0, -1):
        offset = msg_ref[k, samples:base] + c_ref[k, base + 1][None] * e_ref[k]
        t = offset + c_ref[k, base + 2][None] * t
        t_ref[k - 1] = t


def per_device(
    prior_noise,
    kappa_sq,
    horiz_cond,
    vert_cond,
    line_lower,
    line_pivot,
    deflation,
    obs_value,
    obs_weight,
    obs_cell,
    obs_count,
):
    samples = prior_noise.shape[0]
    vectors = deflation.shape[0]
    block_shape = prior_noise.shape[1:]
    layers = block_shape[0]
    cell_count = kappa_sq.size
    f32 = jnp.float32
    sent = jnp.concatenate([obs_value, obs_weight[None]], 0)
    got = lax.all_to_all(sent, "depth", split_axis=3, concat_axis=2, tiled=True)
    got_value, got_weight = got[:samples], got[samples]
    slot_index = lax.broadcasted_iota(jnp.int32, obs_cell.shape[2:], 1)
    live_slot = (slot_index < obs_count[0, 0][:, None]).astype(f32).reshape(-1)
    weights = got_weight.reshape(-1) * live_slot
    targets = obs_cell.reshape(-1)
    obs_diag = jnp.zeros((cell_count,), f32).at[targets].add(weights).reshape(block_shape)
    obs_rhs = (
        jnp.zeros((samples, cell_count), f32)
        .at[:, targets]
        .add(got_value.reshape(samples, -1) * weights[None])
    )
    obs_rhs = obs_rhs.reshape(prior_noise.shape)

    joint = jnp.concatenate(
        [prior_noise, deflation, horiz_cond[None], vert_cond[None]], 0
    )
    j_below, j_above = neighbours(joint, "depth", 1)
    j_rowm, j_rowp = neighbours(joint, "tile", 2)
    lead = samples + vectors
    v_below, v_above = j_below[lead + 1], j_above[lead + 1]
    h_rowm, h_rowp = j_rowm[lead], j_rowp[lead]
    h_colp, h_colm = column_up(horiz_cond), column_down(horiz_cond)
    diag_part = (
        kappa_sq
        + horiz_cond * (h_rowp + h_rowm + h_colp + h_colm)
        + vert_cond * (v_above + v_below)
    )
    c_below, c_above = vert_cond * v_below, vert_cond * v_above
    c_rowm, c_rowp = horiz_cond * h_rowm, horiz_cond * h_rowp
    c_colm, c_colp = horiz_cond * h_colm, horiz_cond * h_colp

    def kcombine(u, below, above, rowm, rowp):
        flux = (
            c_rowp * rowp
            + c_rowm * rowm
            + c_colp * column_up(u)
            + c_colm * column_down(u)
            + c_above * above
            + c_below * below
        )
        return diag_part * u - flux

    def kapply(u):
        below, above = neighbours(u, "depth", 1)
        rowm, rowp = neighbours(u, "tile", 2)
        return kcombine(u, below, above, rowm, rowp)

    field = jax.ShapeDtypeStruct(block_shape, f32)
    gain_down, gain_up, h_field, consts = pl.pallas_call(
        prep_kernel,
        out_shape=(field, field, field, jax.ShapeDtypeStruct((3,) + block_shape[1:], f32)),
    )(line_lower, line_pivot)
    width = 2 * samples

    def line_solve(resid_in, consts_all=None):
        back, message = pl.pallas_call(
            sweep_kernel,
            out_shape=(
                jax.ShapeDtypeStruct(resid_in.shape, f32),
                jax.ShapeDtypeStruct((2, samples) + block_shape[1:], f32),
            ),
        )(resid_in, line_lower, line_pivot)
        message = message.reshape((width,) + block_shape[1:])
        if consts_all is None:
            messages = gather_depth(jnp.concatenate([message, consts], 0))
            consts_all = messages
        else:
            messages = gather_depth(message)
        count = messages.shape[0]
        enter_all, top_all = pl.pallas_call(
            scan_kernel,
            out_shape=(
                jax.ShapeDtypeStruct((count, samples) + block_shape[1:], f32),
                jax.ShapeDtypeStruct((count, samples) + block_shape[1:], f32),
            ),
        )(messages, consts_all)
        mine = lax.axis_index("depth")
        enter = lax.dynamic_index_in_dim(enter_all, mine, 0, keepdims=False)
        top = lax.dynamic_index_in_dim(top_all, mine, 0, keepdims=False)
        result = back + enter[:, None] * h_field[None] + top[:, None] * gain_up[None]
        return result, consts_all

    k_joint = kcombine(
        joint[:lead], j_below[:lead], j_above[:lead], j_rowm[:lead], j_rowp[:lead]
    )
    right_side = k_joint[:samples] + obs_rhs
    basis_flat = deflation.reshape(vectors, cell_count)
    kbasis = k_joint[samples:]
    abasis_flat = (kapply(kbasis) + obs_diag * deflation).reshape(vectors, cell_count)
    gram_part = cells_dot(basis_flat, abasis_flat)
    proj_part = cells_dot(basis_flat, right_side.reshape(samples, cell_count))
    first = all_sum(jnp.concatenate([gram_part.reshape(-1), proj_part.reshape(-1)]))
    gram_total = first[: vectors * vectors].reshape(vectors, vectors)
    proj_rhs = first[vectors * vectors :].reshape(vectors, samples)
    gram_matrix = 0.5 * (gram_total + gram_total.T)
    chol_factor = jnp.linalg.cholesky(gram_matrix)

    def coarse(terms):
        return jax.scipy.linalg.cho_solve((chol_factor, True), terms)

    def expand(rows_flat, coarse_coef):
        return jnp.dot(coarse_coef.T, rows_flat, precision=PRECISE).reshape(prior_noise.shape)

    def inner_sum(left_side, right_part):
        return jnp.sum(left_side * right_part, axis=(1, 2, 3))

    def project(field_in):
        return cells_dot(abasis_flat, field_in.reshape(samples, cell_count))

    coarse_coef = coarse(proj_rhs)
    solution = expand(basis_flat, coarse_coef)
    residual = right_side - expand(abasis_flat, coarse_coef)

    precond, consts_all = line_solve(residual)
    k_precond = kapply(precond)
    sums = all_sum(
        jnp.concatenate(
            [
                inner_sum(residual, precond),
                inner_sum(k_precond, k_precond) + inner_sum(obs_diag * precond, precond),
                project(precond).reshape(-1),
            ]
        )
    )
    rz_now, pap = sums[:samples], sums[samples : 2 * samples]
    proj_now = sums[2 * samples :].reshape(vectors, samples)
    a_precond = kapply(k_precond) + obs_diag * precond
    coarse_dir = coarse(proj_now)
    direction = precond - expand(basis_flat, coarse_dir)
    image_dir = a_precond - expand(abasis_flat, coarse_dir)
    curve_val = pap - jnp.sum(coarse_dir * proj_now, 0)
    step_field = (rz_now / curve_val)[:, None, None, None]
    solution = solution + step_field * direction
    residual = residual - step_field * image_dir

    precond, _ = line_solve(residual, consts_all)
    k_precond = kapply(precond)
    sums = all_sum(
        jnp.concatenate(
            [
                inner_sum(residual, precond),
                inner_sum(k_precond, k_precond) + inner_sum(obs_diag * precond, precond),
                inner_sum(image_dir, precond),
                project(precond).reshape(-1),
                project(direction).reshape(-1),
            ]
        )
    )
    rz_next, pap, cross = sums[:samples], sums[samples : 2 * samples], sums[2 * samples : 3 * samples]
    rest = sums[3 * samples :]
    proj_now = rest[: vectors * samples].reshape(vectors, samples)
    proj_old = rest[vectors * samples :].reshape(vectors, samples)
    a_precond = kapply(k_precond) + obs_diag * precond
    coarse_dir = coarse(proj_now)
    beta = rz_next / rz_now
    beta_ratio = beta[:, None, None, None]
    direction = precond + beta_ratio * direction - expand(basis_flat, coarse_dir)
    image_dir = a_precond + beta_ratio * image_dir - expand(abasis_flat, coarse_dir)
    curve_val = (
        pap
        + 2.0 * beta * cross
        + beta * beta * curve_val
        - jnp.sum(coarse_dir * proj_now, 0)
        - 2.0 * beta * jnp.sum(coarse_dir * proj_old, 0)
    )
    step_field = (rz_next / curve_val)[:, None, None, None]
    solution = solution + step_field * direction
    residual = residual - step_field * image_dir
    return (solution, residual)


def solution(mesh):
    return jax.shard_map(
        per_device,
        mesh=mesh,
        in_specs=(
            P(None, "depth", "tile", None),
            P("depth", "tile", None),
            P("depth", "tile", None),
            P("depth", "tile", None),
            P("depth", "tile", None),
            P("depth", "tile", None),
            P(None, "depth", "tile", None),
            P(None, "tile", "depth", None, None),
            P("tile", "depth", None, None),
            P("tile", "depth", None, None),
            P("tile", "depth", None),
        ),
        out_specs=(P(None, "depth", "tile", None), P(None, "depth", "tile", None)),
        check_vma=False,
    )
```

```python
import jax
import jax.numpy as jnp
from jax import lax
from jax.experimental import pallas as pl
from jax.sharding import PartitionSpec as P

ITERS = 2


PRECISE = lax.Precision.HIGHEST


def xor_round(x, axis, masks):
    count = lax.axis_size(axis)
    parts = [lax.ppermute(x, axis, [(i, i ^ m) for i in range(count)]) for m in masks]
    for part in parts:
        x = x + part
    return x


def all_sum(x):
    x = xor_round(x, "tile", tuple(range(1, lax.axis_size("tile"))))
    count, span = lax.axis_size("depth"), 1
    while span < count:
        radix = 4 if count // span >= 4 else 2
        x = xor_round(x, "depth", tuple(span * j for j in range(1, radix)))
        span *= radix
    return x


def gather_depth(x):
    count = lax.axis_size("depth")
    spread = jnp.broadcast_to(x[None], (count,) + x.shape)
    return lax.all_to_all(spread, "depth", 0, 0, tiled=False)


def neighbours(array, axis, dim):
    count, length = lax.axis_size(axis), array.shape[dim]
    up = [(i, i + 1) for i in range(count - 1)]
    down = [(i + 1, i) for i in range(count - 1)]
    last = lax.slice_in_dim(array, length - 1, length, axis=dim)
    first = lax.slice_in_dim(array, 0, 1, axis=dim)
    before = lax.ppermute(last, axis, up)
    after = lax.ppermute(first, axis, down)
    lower = jnp.concatenate([before, lax.slice_in_dim(array, 0, length - 1, axis=dim)], dim)
    upper = jnp.concatenate([lax.slice_in_dim(array, 1, length, axis=dim), after], dim)
    return lower, upper


def column_up(vector_in):
    return jnp.concatenate([vector_in[..., 1:], jnp.zeros_like(vector_in[..., :1])], -1)


def column_down(vector_in):
    return jnp.concatenate([jnp.zeros_like(vector_in[..., :1]), vector_in[..., :-1]], -1)


def cells_dot(left_rows, right_rows):
    return lax.dot_general(left_rows, right_rows, (((1,), (1,)), ((), ())), precision=PRECISE)


def prep_kernel(low_ref, piv_ref, gd_ref, gu_ref, h_ref, c_ref):
    layers = low_ref.shape[0]
    g = -low_ref[0]
    gd_ref[0] = g
    for i in range(1, layers):
        g = -low_ref[i] * g
        gd_ref[i] = g
    u = jnp.ones_like(g)
    gu_ref[layers - 1] = u
    for i in range(layers - 2, -1, -1):
        u = -low_ref[i + 1] * u
        gu_ref[i] = u
    z = gd_ref[layers - 1] / piv_ref[layers - 1]
    h_ref[layers - 1] = z
    for i in range(layers - 2, -1, -1):
        z = gd_ref[i] / piv_ref[i] - low_ref[i + 1] * z
        h_ref[i] = z
    c_ref[0] = gd_ref[layers - 1]
    c_ref[1] = -low_ref[0] * z
    c_ref[2] = -low_ref[0] * u


def sweep_kernel(r_ref, low_ref, piv_ref, bw_ref, msg_ref):
    layers = r_ref.shape[1]
    y = r_ref[:, 0]
    bw_ref[:, 0] = y / piv_ref[0][None]
    for i in range(1, layers):
        y = r_ref[:, i] - low_ref[i][None] * y
        bw_ref[:, i] = y / piv_ref[i][None]
    msg_ref[0] = y
    z = bw_ref[:, layers - 1]
    for i in range(layers - 2, -1, -1):
        z = bw_ref[:, i] - low_ref[i + 1][None] * z
        bw_ref[:, i] = z
    msg_ref[1] = -low_ref[0][None] * z


def scan_kernel(msg_ref, c_ref, e_ref, t_ref):
    count, samples = msg_ref.shape[0], e_ref.shape[1]
    base = 0
    e = jnp.zeros(e_ref.shape[1:], jnp.float32)
    e_ref[0] = e
    for k in range(count - 1):
        e = msg_ref[k, 0:samples] + c_ref[k, base][None] * e
        e_ref[k + 1] = e
    t = jnp.zeros_like(e)
    t_ref[count - 1] = t
    for k in range(count - 1, 0, -1):
        offset = msg_ref[k, samples : 2 * samples] + c_ref[k, base + 1][None] * e_ref[k]
        t = offset + c_ref[k, base + 2][None] * t
        t_ref[k - 1] = t


def per_device(
    prior_noise,
    kappa_sq,
    horiz_cond,
    vert_cond,
    line_lower,
    line_pivot,
    deflation,
    obs_value,
    obs_weight,
    obs_cell,
    obs_count,
):
    samples = prior_noise.shape[0]
    vectors = deflation.shape[0]
    block_shape = prior_noise.shape[1:]
    layers = block_shape[0]
    cell_count = kappa_sq.size
    f32 = jnp.float32
    sent = jnp.concatenate([obs_value, obs_weight[None]], 0)
    got = lax.all_to_all(sent, "depth", split_axis=3, concat_axis=2, tiled=True)
    got_value, got_weight = got[:samples], got[samples]
    slot_index = lax.broadcasted_iota(jnp.int32, obs_cell.shape[2:], 1)
    live_slot = (slot_index < obs_count[0, 0][:, None]).astype(f32).reshape(-1)
    weights = got_weight.reshape(-1) * live_slot
    targets = obs_cell.reshape(-1)
    planes, cols = cell_count // block_shape[2], block_shape[2]
    plane_hot = (
        lax.broadcasted_iota(jnp.int32, (planes, targets.size), 0) == (targets // cols)[None]
    ).astype(f32)
    col_hot = (
        lax.broadcasted_iota(jnp.int32, (targets.size, cols), 1) == (targets % cols)[:, None]
    ).astype(f32)
    slot_terms = jnp.concatenate([got_value.reshape(samples, -1) * weights[None], weights[None]], 0)
    placed = jnp.einsum(
        "po,joc->jpc", plane_hot, slot_terms[:, :, None] * col_hot[None], precision=PRECISE
    )
    obs_rhs = placed[:samples].reshape(prior_noise.shape)
    obs_diag = placed[samples].reshape(block_shape)

    joint = jnp.concatenate(
        [prior_noise, deflation, horiz_cond[None], vert_cond[None]], 0
    )
    j_below, j_above = neighbours(joint, "depth", 1)
    j_rowm, j_rowp = neighbours(joint, "tile", 2)
    lead = samples + vectors
    v_below, v_above = j_below[lead + 1], j_above[lead + 1]
    h_rowm, h_rowp = j_rowm[lead], j_rowp[lead]
    h_colp, h_colm = column_up(horiz_cond), column_down(horiz_cond)
    diag_part = (
        kappa_sq
        + horiz_cond * (h_rowp + h_rowm + h_colp + h_colm)
        + vert_cond * (v_above + v_below)
    )
    c_below, c_above = vert_cond * v_below, vert_cond * v_above
    c_rowm, c_rowp = horiz_cond * h_rowm, horiz_cond * h_rowp
    c_colm, c_colp = horiz_cond * h_colm, horiz_cond * h_colp

    def kcombine(u, below, above, rowm, rowp):
        flux = (
            c_rowp * rowp
            + c_rowm * rowm
            + c_colp * column_up(u)
            + c_colm * column_down(u)
            + c_above * above
            + c_below * below
        )
        return diag_part * u - flux

    def kapply(u):
        below, above = neighbours(u, "depth", 1)
        rowm, rowp = neighbours(u, "tile", 2)
        return kcombine(u, below, above, rowm, rowp)

    field = jax.ShapeDtypeStruct(block_shape, f32)
    gain_down, gain_up, h_field, consts = pl.pallas_call(
        prep_kernel,
        out_shape=(field, field, field, jax.ShapeDtypeStruct((3,) + block_shape[1:], f32)),
    )(line_lower, line_pivot)
    width = 2 * samples
    consts_all = gather_depth(consts)

    def line_solve(resid_in):
        back, message = pl.pallas_call(
            sweep_kernel,
            out_shape=(
                jax.ShapeDtypeStruct(resid_in.shape, f32),
                jax.ShapeDtypeStruct((2, samples) + block_shape[1:], f32),
            ),
        )(resid_in, line_lower, line_pivot)
        messages = gather_depth(message.reshape((width,) + block_shape[1:]))
        count = messages.shape[0]
        enter_all, top_all = pl.pallas_call(
            scan_kernel,
            out_shape=(
                jax.ShapeDtypeStruct((count, samples) + block_shape[1:], f32),
                jax.ShapeDtypeStruct((count, samples) + block_shape[1:], f32),
            ),
        )(messages, consts_all)
        mine = lax.axis_index("depth")
        enter = lax.dynamic_index_in_dim(enter_all, mine, 0, keepdims=False)
        top = lax.dynamic_index_in_dim(top_all, mine, 0, keepdims=False)
        result = back + enter[:, None] * h_field[None] + top[:, None] * gain_up[None]
        return result

    k_joint = kcombine(
        joint[:lead], j_below[:lead], j_above[:lead], j_rowm[:lead], j_rowp[:lead]
    )
    right_side = k_joint[:samples] + obs_rhs
    basis_flat = deflation.reshape(vectors, cell_count)
    kbasis = k_joint[samples:]
    abasis_flat = (kapply(kbasis) + obs_diag * deflation).reshape(vectors, cell_count)
    gram_part = cells_dot(basis_flat, abasis_flat)
    proj_part = cells_dot(basis_flat, right_side.reshape(samples, cell_count))
    first = all_sum(jnp.concatenate([gram_part.reshape(-1), proj_part.reshape(-1)]))
    gram_total = first[: vectors * vectors].reshape(vectors, vectors)
    proj_rhs = first[vectors * vectors :].reshape(vectors, samples)
    gram_matrix = 0.5 * (gram_total + gram_total.T)
    chol_factor = jnp.linalg.cholesky(gram_matrix)

    def coarse(terms):
        return jax.scipy.linalg.cho_solve((chol_factor, True), terms)

    def expand(rows_flat, coarse_coef):
        return jnp.dot(coarse_coef.T, rows_flat, precision=PRECISE).reshape(prior_noise.shape)

    def inner_sum(left_side, right_part):
        return jnp.sum(left_side * right_part, axis=(1, 2, 3))

    def project(field_in):
        return cells_dot(abasis_flat, field_in.reshape(samples, cell_count))

    coarse_coef = coarse(proj_rhs)
    solution = expand(basis_flat, coarse_coef)
    residual = right_side - expand(abasis_flat, coarse_coef)

    precond = line_solve(residual)
    k_precond = kapply(precond)
    sums = all_sum(
        jnp.concatenate(
            [
                inner_sum(residual, precond),
                inner_sum(k_precond, k_precond) + inner_sum(obs_diag * precond, precond),
                project(precond).reshape(-1),
            ]
        )
    )
    rz_now, pap = sums[:samples], sums[samples : 2 * samples]
    proj_now = sums[2 * samples :].reshape(vectors, samples)
    a_precond = kapply(k_precond) + obs_diag * precond
    coarse_dir = coarse(proj_now)
    direction = precond - expand(basis_flat, coarse_dir)
    image_dir = a_precond - expand(abasis_flat, coarse_dir)
    curve_val = pap - jnp.sum(coarse_dir * proj_now, 0)
    step_field = (rz_now / curve_val)[:, None, None, None]
    solution = solution + step_field * direction
    residual = residual - step_field * image_dir

    precond = line_solve(residual)
    k_precond = kapply(precond)
    sums = all_sum(
        jnp.concatenate(
            [
                inner_sum(residual, precond),
                inner_sum(k_precond, k_precond) + inner_sum(obs_diag * precond, precond),
                inner_sum(image_dir, precond),
                project(precond).reshape(-1),
                project(direction).reshape(-1),
            ]
        )
    )
    rz_next, pap, cross = sums[:samples], sums[samples : 2 * samples], sums[2 * samples : 3 * samples]
    rest = sums[3 * samples :]
    proj_now = rest[: vectors * samples].reshape(vectors, samples)
    proj_old = rest[vectors * samples :].reshape(vectors, samples)
    a_precond = kapply(k_precond) + obs_diag * precond
    coarse_dir = coarse(proj_now)
    beta = rz_next / rz_now
    beta_ratio = beta[:, None, None, None]
    direction = precond + beta_ratio * direction - expand(basis_flat, coarse_dir)
    image_dir = a_precond + beta_ratio * image_dir - expand(abasis_flat, coarse_dir)
    curve_val = (
        pap
        + 2.0 * beta * cross
        + beta * beta * curve_val
        - jnp.sum(coarse_dir * proj_now, 0)
        - 2.0 * beta * jnp.sum(coarse_dir * proj_old, 0)
    )
    step_field = (rz_next / curve_val)[:, None, None, None]
    solution = solution + step_field * direction
    residual = residual - step_field * image_dir
    return (solution, residual)


def solution(mesh):
    return jax.shard_map(
        per_device,
        mesh=mesh,
        in_specs=(
            P(None, "depth", "tile", None),
            P("depth", "tile", None),
            P("depth", "tile", None),
            P("depth", "tile", None),
            P("depth", "tile", None),
            P("depth", "tile", None),
            P(None, "depth", "tile", None),
            P(None, "tile", "depth", None, None),
            P("tile", "depth", None, None),
            P("tile", "depth", None, None),
            P("tile", "depth", None),
        ),
        out_specs=(P(None, "depth", "tile", None), P(None, "depth", "tile", None)),
        check_vma=False,
    )
```

```python
import jax
import jax.numpy as jnp
from jax import lax
from jax.experimental import pallas as pl
from jax.sharding import PartitionSpec as P

ITERS = 2


PRECISE = lax.Precision.HIGHEST


def all_sum(x):
    count = lax.axis_size("tile") * lax.axis_size("depth")
    spread = jnp.broadcast_to(x[None], (count,) + x.shape)
    return jnp.sum(lax.all_to_all(spread, ("tile", "depth"), 0, 0, tiled=False), 0)


def gather_depth(x):
    count = lax.axis_size("depth")
    spread = jnp.broadcast_to(x[None], (count,) + x.shape)
    return lax.all_to_all(spread, "depth", 0, 0, tiled=False)


def neighbours(array, axis, dim):
    count, length = lax.axis_size(axis), array.shape[dim]
    up = [(i, i + 1) for i in range(count - 1)]
    down = [(i + 1, i) for i in range(count - 1)]
    last = lax.slice_in_dim(array, length - 1, length, axis=dim)
    first = lax.slice_in_dim(array, 0, 1, axis=dim)
    before = lax.ppermute(last, axis, up)
    after = lax.ppermute(first, axis, down)
    lower = jnp.concatenate([before, lax.slice_in_dim(array, 0, length - 1, axis=dim)], dim)
    upper = jnp.concatenate([lax.slice_in_dim(array, 1, length, axis=dim), after], dim)
    return lower, upper


def column_up(vector_in):
    return jnp.concatenate([vector_in[..., 1:], jnp.zeros_like(vector_in[..., :1])], -1)


def column_down(vector_in):
    return jnp.concatenate([jnp.zeros_like(vector_in[..., :1]), vector_in[..., :-1]], -1)


def cells_dot(left_rows, right_rows):
    return lax.dot_general(left_rows, right_rows, (((1,), (1,)), ((), ())), precision=PRECISE)


def prep_kernel(low_ref, piv_ref, gd_ref, gu_ref, h_ref, c_ref):
    layers = low_ref.shape[0]
    g = -low_ref[0]
    gd_ref[0] = g
    for i in range(1, layers):
        g = -low_ref[i] * g
        gd_ref[i] = g
    u = jnp.ones_like(g)
    gu_ref[layers - 1] = u
    for i in range(layers - 2, -1, -1):
        u = -low_ref[i + 1] * u
        gu_ref[i] = u
    z = gd_ref[layers - 1] / piv_ref[layers - 1]
    h_ref[layers - 1] = z
    for i in range(layers - 2, -1, -1):
        z = gd_ref[i] / piv_ref[i] - low_ref[i + 1] * z
        h_ref[i] = z
    c_ref[0] = gd_ref[layers - 1]
    c_ref[1] = -low_ref[0] * z
    c_ref[2] = -low_ref[0] * u


def sweep_kernel(r_ref, low_ref, piv_ref, bw_ref, msg_ref):
    layers = r_ref.shape[1]
    y = r_ref[:, 0]
    bw_ref[:, 0] = y / piv_ref[0][None]
    for i in range(1, layers):
        y = r_ref[:, i] - low_ref[i][None] * y
        bw_ref[:, i] = y / piv_ref[i][None]
    msg_ref[0] = y
    z = bw_ref[:, layers - 1]
    for i in range(layers - 2, -1, -1):
        z = bw_ref[:, i] - low_ref[i + 1][None] * z
        bw_ref[:, i] = z
    msg_ref[1] = -low_ref[0][None] * z


def scan_kernel(msg_ref, c_ref, e_ref, t_ref):
    count, samples = msg_ref.shape[0], e_ref.shape[1]
    base = 2 * samples
    e = jnp.zeros(e_ref.shape[1:], jnp.float32)
    e_ref[0] = e
    for k in range(count - 1):
        e = msg_ref[k, 0:samples] + c_ref[k, base][None] * e
        e_ref[k + 1] = e
    t = jnp.zeros_like(e)
    t_ref[count - 1] = t
    for k in range(count - 1, 0, -1):
        offset = msg_ref[k, samples : 2 * samples] + c_ref[k, base + 1][None] * e_ref[k]
        t = offset + c_ref[k, base + 2][None] * t
        t_ref[k - 1] = t


def per_device(
    prior_noise,
    kappa_sq,
    horiz_cond,
    vert_cond,
    line_lower,
    line_pivot,
    deflation,
    obs_value,
    obs_weight,
    obs_cell,
    obs_count,
):
    samples = prior_noise.shape[0]
    vectors = deflation.shape[0]
    block_shape = prior_noise.shape[1:]
    layers = block_shape[0]
    cell_count = kappa_sq.size
    f32 = jnp.float32
    sent = jnp.concatenate([obs_value, obs_weight[None]], 0)
    got = lax.all_to_all(sent, "depth", split_axis=3, concat_axis=2, tiled=True)
    got_value, got_weight = got[:samples], got[samples]
    slot_index = lax.broadcasted_iota(jnp.int32, obs_cell.shape[2:], 1)
    live_slot = (slot_index < obs_count[0, 0][:, None]).astype(f32).reshape(-1)
    weights = got_weight.reshape(-1) * live_slot
    targets = obs_cell.reshape(-1)
    planes, cols = cell_count // block_shape[2], block_shape[2]
    plane_hot = (
        lax.broadcasted_iota(jnp.int32, (planes, targets.size), 0) == (targets // cols)[None]
    ).astype(f32)
    col_hot = (
        lax.broadcasted_iota(jnp.int32, (targets.size, cols), 1) == (targets % cols)[:, None]
    ).astype(f32)
    slot_terms = jnp.concatenate([got_value.reshape(samples, -1) * weights[None], weights[None]], 0)
    placed = jnp.einsum(
        "po,joc->jpc", plane_hot, slot_terms[:, :, None] * col_hot[None], precision=PRECISE
    )
    obs_rhs = placed[:samples].reshape(prior_noise.shape)
    obs_diag = placed[samples].reshape(block_shape)

    joint = jnp.concatenate(
        [prior_noise, deflation, horiz_cond[None], vert_cond[None]], 0
    )
    j_below, j_above = neighbours(joint, "depth", 1)
    j_rowm, j_rowp = neighbours(joint, "tile", 2)
    lead = samples + vectors
    v_below, v_above = j_below[lead + 1], j_above[lead + 1]
    h_rowm, h_rowp = j_rowm[lead], j_rowp[lead]
    h_colp, h_colm = column_up(horiz_cond), column_down(horiz_cond)
    diag_part = (
        kappa_sq
        + horiz_cond * (h_rowp + h_rowm + h_colp + h_colm)
        + vert_cond * (v_above + v_below)
    )
    c_below, c_above = vert_cond * v_below, vert_cond * v_above
    c_rowm, c_rowp = horiz_cond * h_rowm, horiz_cond * h_rowp
    c_colm, c_colp = horiz_cond * h_colm, horiz_cond * h_colp

    def kcombine(u, below, above, rowm, rowp):
        flux = (
            c_rowp * rowp
            + c_rowm * rowm
            + c_colp * column_up(u)
            + c_colm * column_down(u)
            + c_above * above
            + c_below * below
        )
        return diag_part * u - flux

    def kapply(u):
        below, above = neighbours(u, "depth", 1)
        rowm, rowp = neighbours(u, "tile", 2)
        return kcombine(u, below, above, rowm, rowp)

    field = jax.ShapeDtypeStruct(block_shape, f32)
    gain_down, gain_up, h_field, consts = pl.pallas_call(
        prep_kernel,
        out_shape=(field, field, field, jax.ShapeDtypeStruct((3,) + block_shape[1:], f32)),
    )(line_lower, line_pivot)
    width = 2 * samples

    def line_solve(resid_in, consts_all=None):
        back, message = pl.pallas_call(
            sweep_kernel,
            out_shape=(
                jax.ShapeDtypeStruct(resid_in.shape, f32),
                jax.ShapeDtypeStruct((2, samples) + block_shape[1:], f32),
            ),
        )(resid_in, line_lower, line_pivot)
        message = message.reshape((width,) + block_shape[1:])
        if consts_all is None:
            messages = gather_depth(jnp.concatenate([message, consts], 0))
            consts_all = messages
        else:
            messages = gather_depth(message)
        count = messages.shape[0]
        enter_all, top_all = pl.pallas_call(
            scan_kernel,
            out_shape=(
                jax.ShapeDtypeStruct((count, samples) + block_shape[1:], f32),
                jax.ShapeDtypeStruct((count, samples) + block_shape[1:], f32),
            ),
        )(messages, consts_all)
        mine = lax.axis_index("depth")
        enter = lax.dynamic_index_in_dim(enter_all, mine, 0, keepdims=False)
        top = lax.dynamic_index_in_dim(top_all, mine, 0, keepdims=False)
        result = back + enter[:, None] * h_field[None] + top[:, None] * gain_up[None]
        return result, consts_all

    k_joint = kcombine(
        joint[:lead], j_below[:lead], j_above[:lead], j_rowm[:lead], j_rowp[:lead]
    )
    right_side = k_joint[:samples] + obs_rhs
    basis_flat = deflation.reshape(vectors, cell_count)
    kbasis = k_joint[samples:]
    abasis_flat = (kapply(kbasis) + obs_diag * deflation).reshape(vectors, cell_count)
    gram_part = cells_dot(basis_flat, abasis_flat)
    proj_part = cells_dot(basis_flat, right_side.reshape(samples, cell_count))
    first = all_sum(jnp.concatenate([gram_part.reshape(-1), proj_part.reshape(-1)]))
    gram_total = first[: vectors * vectors].reshape(vectors, vectors)
    proj_rhs = first[vectors * vectors :].reshape(vectors, samples)
    gram_matrix = 0.5 * (gram_total + gram_total.T)
    chol_factor = jnp.linalg.cholesky(gram_matrix)

    def coarse(terms):
        return jax.scipy.linalg.cho_solve((chol_factor, True), terms)

    def expand(rows_flat, coarse_coef):
        return jnp.dot(coarse_coef.T, rows_flat, precision=PRECISE).reshape(prior_noise.shape)

    def inner_sum(left_side, right_part):
        return jnp.sum(left_side * right_part, axis=(1, 2, 3))

    def project(field_in):
        return cells_dot(abasis_flat, field_in.reshape(samples, cell_count))

    coarse_coef = coarse(proj_rhs)
    solution = expand(basis_flat, coarse_coef)
    residual = right_side - expand(abasis_flat, coarse_coef)

    precond, consts_all = line_solve(residual)
    k_precond = kapply(precond)
    sums = all_sum(
        jnp.concatenate(
            [
                inner_sum(residual, precond),
                inner_sum(k_precond, k_precond) + inner_sum(obs_diag * precond, precond),
                project(precond).reshape(-1),
            ]
        )
    )
    rz_now, pap = sums[:samples], sums[samples : 2 * samples]
    proj_now = sums[2 * samples :].reshape(vectors, samples)
    a_precond = kapply(k_precond) + obs_diag * precond
    coarse_dir = coarse(proj_now)
    direction = precond - expand(basis_flat, coarse_dir)
    image_dir = a_precond - expand(abasis_flat, coarse_dir)
    curve_val = pap - jnp.sum(coarse_dir * proj_now, 0)
    step_field = (rz_now / curve_val)[:, None, None, None]
    solution = solution + step_field * direction
    residual = residual - step_field * image_dir

    precond, _ = line_solve(residual, consts_all)
    k_precond = kapply(precond)
    sums = all_sum(
        jnp.concatenate(
            [
                inner_sum(residual, precond),
                inner_sum(k_precond, k_precond) + inner_sum(obs_diag * precond, precond),
                inner_sum(image_dir, precond),
                project(precond).reshape(-1),
                project(direction).reshape(-1),
            ]
        )
    )
    rz_next, pap, cross = sums[:samples], sums[samples : 2 * samples], sums[2 * samples : 3 * samples]
    rest = sums[3 * samples :]
    proj_now = rest[: vectors * samples].reshape(vectors, samples)
    proj_old = rest[vectors * samples :].reshape(vectors, samples)
    a_precond = kapply(k_precond) + obs_diag * precond
    coarse_dir = coarse(proj_now)
    beta = rz_next / rz_now
    beta_ratio = beta[:, None, None, None]
    direction = precond + beta_ratio * direction - expand(basis_flat, coarse_dir)
    image_dir = a_precond + beta_ratio * image_dir - expand(abasis_flat, coarse_dir)
    curve_val = (
        pap
        + 2.0 * beta * cross
        + beta * beta * curve_val
        - jnp.sum(coarse_dir * proj_now, 0)
        - 2.0 * beta * jnp.sum(coarse_dir * proj_old, 0)
    )
    step_field = (rz_next / curve_val)[:, None, None, None]
    solution = solution + step_field * direction
    residual = residual - step_field * image_dir
    return (solution, residual)


def solution(mesh):
    return jax.shard_map(
        per_device,
        mesh=mesh,
        in_specs=(
            P(None, "depth", "tile", None),
            P("depth", "tile", None),
            P("depth", "tile", None),
            P("depth", "tile", None),
            P("depth", "tile", None),
            P("depth", "tile", None),
            P(None, "depth", "tile", None),
            P(None, "tile", "depth", None, None),
            P("tile", "depth", None, None),
            P("tile", "depth", None, None),
            P("tile", "depth", None),
        ),
        out_specs=(P(None, "depth", "tile", None), P(None, "depth", "tile", None)),
        check_vma=False,
    )
```

```python
import jax
import jax.numpy as jnp
from jax import lax
from jax.experimental import pallas as pl
from jax.sharding import PartitionSpec as P

ITERS = 2


PRECISE = lax.Precision.HIGHEST


def all_sum(x):
    count = lax.axis_size("tile") * lax.axis_size("depth")
    spread = jnp.broadcast_to(x[None], (count,) + x.shape)
    return jnp.sum(lax.all_to_all(spread, ("tile", "depth"), 0, 0, tiled=False), 0)


def gather_depth(x):
    count = lax.axis_size("depth")
    spread = jnp.broadcast_to(x[None], (count,) + x.shape)
    return lax.all_to_all(spread, "depth", 0, 0, tiled=False)


def neighbours(array, axis, dim):
    count, length = lax.axis_size(axis), array.shape[dim]
    up = [(i, i + 1) for i in range(count - 1)]
    down = [(i + 1, i) for i in range(count - 1)]
    last = lax.slice_in_dim(array, length - 1, length, axis=dim)
    first = lax.slice_in_dim(array, 0, 1, axis=dim)
    before = lax.ppermute(last, axis, up)
    after = lax.ppermute(first, axis, down)
    lower = jnp.concatenate([before, lax.slice_in_dim(array, 0, length - 1, axis=dim)], dim)
    upper = jnp.concatenate([lax.slice_in_dim(array, 1, length, axis=dim), after], dim)
    return lower, upper


def column_up(vector_in):
    return jnp.concatenate([vector_in[..., 1:], jnp.zeros_like(vector_in[..., :1])], -1)


def column_down(vector_in):
    return jnp.concatenate([jnp.zeros_like(vector_in[..., :1]), vector_in[..., :-1]], -1)


def cells_dot(left_rows, right_rows):
    return lax.dot_general(left_rows, right_rows, (((1,), (1,)), ((), ())), precision=PRECISE)


def prep_kernel(low_ref, piv_ref, gd_ref, gu_ref, h_ref, c_ref):
    layers = low_ref.shape[0]
    g = -low_ref[0]
    gd_ref[0] = g
    for i in range(1, layers):
        g = -low_ref[i] * g
        gd_ref[i] = g
    u = jnp.ones_like(g)
    gu_ref[layers - 1] = u
    for i in range(layers - 2, -1, -1):
        u = -low_ref[i + 1] * u
        gu_ref[i] = u
    z = gd_ref[layers - 1] / piv_ref[layers - 1]
    h_ref[layers - 1] = z
    for i in range(layers - 2, -1, -1):
        z = gd_ref[i] / piv_ref[i] - low_ref[i + 1] * z
        h_ref[i] = z
    c_ref[0] = gd_ref[layers - 1]
    c_ref[1] = -low_ref[0] * z
    c_ref[2] = -low_ref[0] * u


def sweep_kernel(r_ref, low_ref, piv_ref, bw_ref, msg_ref):
    layers = r_ref.shape[1]
    y = r_ref[:, 0]
    bw_ref[:, 0] = y / piv_ref[0][None]
    for i in range(1, layers):
        y = r_ref[:, i] - low_ref[i][None] * y
        bw_ref[:, i] = y / piv_ref[i][None]
    msg_ref[0] = y
    z = bw_ref[:, layers - 1]
    for i in range(layers - 2, -1, -1):
        z = bw_ref[:, i] - low_ref[i + 1][None] * z
        bw_ref[:, i] = z
    msg_ref[1] = -low_ref[0][None] * z


def scan_kernel(msg_ref, c_ref, e_ref, t_ref):
    count, samples = msg_ref.shape[0], e_ref.shape[1]
    base = 0
    e = jnp.zeros(e_ref.shape[1:], jnp.float32)
    e_ref[0] = e
    for k in range(count - 1):
        e = msg_ref[k, 0:samples] + c_ref[k, base][None] * e
        e_ref[k + 1] = e
    t = jnp.zeros_like(e)
    t_ref[count - 1] = t
    for k in range(count - 1, 0, -1):
        offset = msg_ref[k, samples : 2 * samples] + c_ref[k, base + 1][None] * e_ref[k]
        t = offset + c_ref[k, base + 2][None] * t
        t_ref[k - 1] = t


def per_device(
    prior_noise,
    kappa_sq,
    horiz_cond,
    vert_cond,
    line_lower,
    line_pivot,
    deflation,
    obs_value,
    obs_weight,
    obs_cell,
    obs_count,
):
    samples = prior_noise.shape[0]
    vectors = deflation.shape[0]
    block_shape = prior_noise.shape[1:]
    layers = block_shape[0]
    cell_count = kappa_sq.size
    f32 = jnp.float32
    field = jax.ShapeDtypeStruct(block_shape, f32)
    gain_down, gain_up, h_field, consts = pl.pallas_call(
        prep_kernel,
        out_shape=(field, field, field, jax.ShapeDtypeStruct((3,) + block_shape[1:], f32)),
    )(line_lower, line_pivot)
    count = lax.axis_size("depth")
    value_rows = jnp.transpose(obs_value[:, 0, 0], (1, 0, 2)).reshape(count, -1)
    obs_rows = jnp.concatenate([value_rows, obs_weight[0, 0]], 1)
    const_rows = jnp.broadcast_to(consts.reshape(1, -1), (count, consts.size))
    got = lax.all_to_all(
        jnp.concatenate([obs_rows, const_rows], 1), "depth", 0, 0, tiled=False
    )
    slots = obs_rows.shape[1] // (samples + 1)
    got_value = jnp.transpose(got[:, : samples * slots].reshape(count, samples, slots), (1, 0, 2))
    got_weight = got[:, samples * slots : obs_rows.shape[1]]
    consts_all = got[:, obs_rows.shape[1] :].reshape((count,) + consts.shape)
    slot_index = lax.broadcasted_iota(jnp.int32, obs_cell.shape[2:], 1)
    live_slot = (slot_index < obs_count[0, 0][:, None]).astype(f32).reshape(-1)
    weights = got_weight.reshape(-1) * live_slot
    targets = obs_cell.reshape(-1)
    planes, cols = cell_count // block_shape[2], block_shape[2]
    plane_hot = (
        lax.broadcasted_iota(jnp.int32, (planes, targets.size), 0) == (targets // cols)[None]
    ).astype(f32)
    col_hot = (
        lax.broadcasted_iota(jnp.int32, (targets.size, cols), 1) == (targets % cols)[:, None]
    ).astype(f32)
    slot_terms = jnp.concatenate([got_value.reshape(samples, -1) * weights[None], weights[None]], 0)
    placed = jnp.einsum(
        "po,joc->jpc", plane_hot, slot_terms[:, :, None] * col_hot[None], precision=PRECISE
    )
    obs_rhs = placed[:samples].reshape(prior_noise.shape)
    obs_diag = placed[samples].reshape(block_shape)

    joint = jnp.concatenate(
        [prior_noise, deflation, horiz_cond[None], vert_cond[None]], 0
    )
    j_below, j_above = neighbours(joint, "depth", 1)
    j_rowm, j_rowp = neighbours(joint, "tile", 2)
    lead = samples + vectors
    v_below, v_above = j_below[lead + 1], j_above[lead + 1]
    h_rowm, h_rowp = j_rowm[lead], j_rowp[lead]
    h_colp, h_colm = column_up(horiz_cond), column_down(horiz_cond)
    diag_part = (
        kappa_sq
        + horiz_cond * (h_rowp + h_rowm + h_colp + h_colm)
        + vert_cond * (v_above + v_below)
    )
    c_below, c_above = vert_cond * v_below, vert_cond * v_above
    c_rowm, c_rowp = horiz_cond * h_rowm, horiz_cond * h_rowp
    c_colm, c_colp = horiz_cond * h_colm, horiz_cond * h_colp

    def kcombine(u, below, above, rowm, rowp):
        flux = (
            c_rowp * rowp
            + c_rowm * rowm
            + c_colp * column_up(u)
            + c_colm * column_down(u)
            + c_above * above
            + c_below * below
        )
        return diag_part * u - flux

    def kapply(u):
        below, above = neighbours(u, "depth", 1)
        rowm, rowp = neighbours(u, "tile", 2)
        return kcombine(u, below, above, rowm, rowp)

    width = 2 * samples

    def line_solve(resid_in):
        back, message = pl.pallas_call(
            sweep_kernel,
            out_shape=(
                jax.ShapeDtypeStruct(resid_in.shape, f32),
                jax.ShapeDtypeStruct((2, samples) + block_shape[1:], f32),
            ),
        )(resid_in, line_lower, line_pivot)
        messages = gather_depth(message.reshape((width,) + block_shape[1:]))
        count = messages.shape[0]
        enter_all, top_all = pl.pallas_call(
            scan_kernel,
            out_shape=(
                jax.ShapeDtypeStruct((count, samples) + block_shape[1:], f32),
                jax.ShapeDtypeStruct((count, samples) + block_shape[1:], f32),
            ),
        )(messages, consts_all)
        mine = lax.axis_index("depth")
        enter = lax.dynamic_index_in_dim(enter_all, mine, 0, keepdims=False)
        top = lax.dynamic_index_in_dim(top_all, mine, 0, keepdims=False)
        result = back + enter[:, None] * h_field[None] + top[:, None] * gain_up[None]
        return result

    k_joint = kcombine(
        joint[:lead], j_below[:lead], j_above[:lead], j_rowm[:lead], j_rowp[:lead]
    )
    right_side = k_joint[:samples] + obs_rhs
    basis_flat = deflation.reshape(vectors, cell_count)
    kbasis = k_joint[samples:]
    abasis_flat = (kapply(kbasis) + obs_diag * deflation).reshape(vectors, cell_count)
    gram_part = cells_dot(basis_flat, abasis_flat)
    proj_part = cells_dot(basis_flat, right_side.reshape(samples, cell_count))
    first = all_sum(jnp.concatenate([gram_part.reshape(-1), proj_part.reshape(-1)]))
    gram_total = first[: vectors * vectors].reshape(vectors, vectors)
    proj_rhs = first[vectors * vectors :].reshape(vectors, samples)
    gram_matrix = 0.5 * (gram_total + gram_total.T)
    chol_factor = jnp.linalg.cholesky(gram_matrix)

    def coarse(terms):
        return jax.scipy.linalg.cho_solve((chol_factor, True), terms)

    def expand(rows_flat, coarse_coef):
        return jnp.dot(coarse_coef.T, rows_flat, precision=PRECISE).reshape(prior_noise.shape)

    def inner_sum(left_side, right_part):
        return jnp.sum(left_side * right_part, axis=(1, 2, 3))

    def project(field_in):
        return cells_dot(abasis_flat, field_in.reshape(samples, cell_count))

    coarse_coef = coarse(proj_rhs)
    solution = expand(basis_flat, coarse_coef)
    residual = right_side - expand(abasis_flat, coarse_coef)

    precond = line_solve(residual)
    k_precond = kapply(precond)
    sums = all_sum(
        jnp.concatenate(
            [
                inner_sum(residual, precond),
                inner_sum(k_precond, k_precond) + inner_sum(obs_diag * precond, precond),
                project(precond).reshape(-1),
            ]
        )
    )
    rz_now, pap = sums[:samples], sums[samples : 2 * samples]
    proj_now = sums[2 * samples :].reshape(vectors, samples)
    a_precond = kapply(k_precond) + obs_diag * precond
    coarse_dir = coarse(proj_now)
    direction = precond - expand(basis_flat, coarse_dir)
    image_dir = a_precond - expand(abasis_flat, coarse_dir)
    curve_val = pap - jnp.sum(coarse_dir * proj_now, 0)
    step_field = (rz_now / curve_val)[:, None, None, None]
    solution = solution + step_field * direction
    residual = residual - step_field * image_dir

    precond = line_solve(residual)
    k_precond = kapply(precond)
    sums = all_sum(
        jnp.concatenate(
            [
                inner_sum(residual, precond),
                inner_sum(k_precond, k_precond) + inner_sum(obs_diag * precond, precond),
                inner_sum(image_dir, precond),
                project(precond).reshape(-1),
                project(direction).reshape(-1),
            ]
        )
    )
    rz_next, pap, cross = sums[:samples], sums[samples : 2 * samples], sums[2 * samples : 3 * samples]
    rest = sums[3 * samples :]
    proj_now = rest[: vectors * samples].reshape(vectors, samples)
    proj_old = rest[vectors * samples :].reshape(vectors, samples)
    a_precond = kapply(k_precond) + obs_diag * precond
    coarse_dir = coarse(proj_now)
    beta = rz_next / rz_now
    beta_ratio = beta[:, None, None, None]
    direction = precond + beta_ratio * direction - expand(basis_flat, coarse_dir)
    image_dir = a_precond + beta_ratio * image_dir - expand(abasis_flat, coarse_dir)
    curve_val = (
        pap
        + 2.0 * beta * cross
        + beta * beta * curve_val
        - jnp.sum(coarse_dir * proj_now, 0)
        - 2.0 * beta * jnp.sum(coarse_dir * proj_old, 0)
    )
    step_field = (rz_next / curve_val)[:, None, None, None]
    solution = solution + step_field * direction
    residual = residual - step_field * image_dir
    return (solution, residual)


def solution(mesh):
    return jax.shard_map(
        per_device,
        mesh=mesh,
        in_specs=(
            P(None, "depth", "tile", None),
            P("depth", "tile", None),
            P("depth", "tile", None),
            P("depth", "tile", None),
            P("depth", "tile", None),
            P("depth", "tile", None),
            P(None, "depth", "tile", None),
            P(None, "tile", "depth", None, None),
            P("tile", "depth", None, None),
            P("tile", "depth", None, None),
            P("tile", "depth", None),
        ),
        out_specs=(P(None, "depth", "tile", None), P(None, "depth", "tile", None)),
        check_vma=False,
    )
```

```python
import jax
import jax.numpy as jnp
from jax import lax
from jax.experimental import pallas as pl
from jax.sharding import PartitionSpec as P

ITERS = 2


PRECISE = lax.Precision.HIGHEST


def all_sum(x):
    count = lax.axis_size("tile") * lax.axis_size("depth")
    spread = jnp.broadcast_to(x[None], (count,) + x.shape)
    return jnp.sum(lax.all_to_all(spread, ("tile", "depth"), 0, 0, tiled=False), 0)


def gather_depth(x):
    count = lax.axis_size("depth")
    spread = jnp.broadcast_to(x[None], (count,) + x.shape)
    return lax.all_to_all(spread, "depth", 0, 0, tiled=False)


def neighbours(array, axis, dim):
    count, length = lax.axis_size(axis), array.shape[dim]
    up = [(i, i + 1) for i in range(count - 1)]
    down = [(i + 1, i) for i in range(count - 1)]
    last = lax.slice_in_dim(array, length - 1, length, axis=dim)
    first = lax.slice_in_dim(array, 0, 1, axis=dim)
    before = lax.ppermute(last, axis, up)
    after = lax.ppermute(first, axis, down)
    lower = jnp.concatenate([before, lax.slice_in_dim(array, 0, length - 1, axis=dim)], dim)
    upper = jnp.concatenate([lax.slice_in_dim(array, 1, length, axis=dim), after], dim)
    return lower, upper


def column_up(vector_in):
    return jnp.concatenate([vector_in[..., 1:], jnp.zeros_like(vector_in[..., :1])], -1)


def column_down(vector_in):
    return jnp.concatenate([jnp.zeros_like(vector_in[..., :1]), vector_in[..., :-1]], -1)


def cells_dot(left_rows, right_rows):
    return lax.dot_general(left_rows, right_rows, (((1,), (1,)), ((), ())), precision=PRECISE)


def prep_kernel(low_ref, piv_ref, gd_ref, gu_ref, h_ref, c_ref):
    layers = low_ref.shape[0]
    g = -low_ref[0]
    gd_ref[0] = g
    for i in range(1, layers):
        g = -low_ref[i] * g
        gd_ref[i] = g
    u = jnp.ones_like(g)
    gu_ref[layers - 1] = u
    for i in range(layers - 2, -1, -1):
        u = -low_ref[i + 1] * u
        gu_ref[i] = u
    z = gd_ref[layers - 1] / piv_ref[layers - 1]
    h_ref[layers - 1] = z
    for i in range(layers - 2, -1, -1):
        z = gd_ref[i] / piv_ref[i] - low_ref[i + 1] * z
        h_ref[i] = z
    c_ref[0] = gd_ref[layers - 1]
    c_ref[1] = -low_ref[0] * z
    c_ref[2] = -low_ref[0] * u


def sweep_kernel(r_ref, low_ref, piv_ref, bw_ref, msg_ref):
    layers = r_ref.shape[1]
    y = r_ref[:, 0]
    bw_ref[:, 0] = y / piv_ref[0][None]
    for i in range(1, layers):
        y = r_ref[:, i] - low_ref[i][None] * y
        bw_ref[:, i] = y / piv_ref[i][None]
    msg_ref[0] = y
    z = bw_ref[:, layers - 1]
    for i in range(layers - 2, -1, -1):
        z = bw_ref[:, i] - low_ref[i + 1][None] * z
        bw_ref[:, i] = z
    msg_ref[1] = -low_ref[0][None] * z


def scan_kernel(msg_ref, c_ref, e_ref, t_ref):
    count, samples = msg_ref.shape[0], e_ref.shape[1]
    base = 0
    e = jnp.zeros(e_ref.shape[1:], jnp.float32)
    e_ref[0] = e
    for k in range(count - 1):
        e = msg_ref[k, 0:samples] + c_ref[k, base][None] * e
        e_ref[k + 1] = e
    t = jnp.zeros_like(e)
    t_ref[count - 1] = t
    for k in range(count - 1, 0, -1):
        offset = msg_ref[k, samples : 2 * samples] + c_ref[k, base + 1][None] * e_ref[k]
        t = offset + c_ref[k, base + 2][None] * t
        t_ref[k - 1] = t


def per_device(
    prior_noise,
    kappa_sq,
    horiz_cond,
    vert_cond,
    line_lower,
    line_pivot,
    deflation,
    obs_value,
    obs_weight,
    obs_cell,
    obs_count,
):
    samples = prior_noise.shape[0]
    vectors = deflation.shape[0]
    block_shape = prior_noise.shape[1:]
    layers = block_shape[0]
    cell_count = kappa_sq.size
    f32 = jnp.float32
    field = jax.ShapeDtypeStruct(block_shape, f32)
    gain_down, gain_up, h_field, consts = pl.pallas_call(
        prep_kernel,
        out_shape=(field, field, field, jax.ShapeDtypeStruct((3,) + block_shape[1:], f32)),
    )(line_lower, line_pivot)
    count = lax.axis_size("depth")
    value_rows = jnp.transpose(obs_value[:, 0, 0], (1, 0, 2)).reshape(count, -1)
    obs_rows = jnp.concatenate([value_rows, obs_weight[0, 0]], 1)
    const_rows = jnp.broadcast_to(consts.reshape(1, -1), (count, consts.size))
    got = lax.all_to_all(
        jnp.concatenate([obs_rows, const_rows], 1), "depth", 0, 0, tiled=False
    )
    slots = obs_rows.shape[1] // (samples + 1)
    got_value = jnp.transpose(got[:, : samples * slots].reshape(count, samples, slots), (1, 0, 2))
    got_weight = got[:, samples * slots : obs_rows.shape[1]]
    consts_all = got[:, obs_rows.shape[1] :].reshape((count,) + consts.shape)
    slot_index = lax.broadcasted_iota(jnp.int32, obs_cell.shape[2:], 1)
    live_slot = (slot_index < obs_count[0, 0][:, None]).astype(f32).reshape(-1)
    weights = got_weight.reshape(-1) * live_slot
    targets = obs_cell.reshape(-1)
    planes, cols = cell_count // block_shape[2], block_shape[2]
    plane_hot = (
        lax.broadcasted_iota(jnp.int32, (planes, targets.size), 0) == (targets // cols)[None]
    ).astype(f32)
    col_hot = (
        lax.broadcasted_iota(jnp.int32, (targets.size, cols), 1) == (targets % cols)[:, None]
    ).astype(f32)
    slot_terms = jnp.concatenate([got_value.reshape(samples, -1) * weights[None], weights[None]], 0)
    placed = jnp.einsum(
        "po,joc->jpc", plane_hot, slot_terms[:, :, None] * col_hot[None], precision=PRECISE
    )
    obs_rhs = placed[:samples].reshape(prior_noise.shape)
    obs_diag = placed[samples].reshape(block_shape)

    joint = jnp.concatenate(
        [prior_noise, deflation, horiz_cond[None], vert_cond[None]], 0
    )
    j_below, j_above = neighbours(joint, "depth", 1)
    j_rowm, j_rowp = neighbours(joint, "tile", 2)
    lead = samples + vectors
    v_below, v_above = j_below[lead + 1], j_above[lead + 1]
    h_rowm, h_rowp = j_rowm[lead], j_rowp[lead]
    h_colp, h_colm = column_up(horiz_cond), column_down(horiz_cond)
    diag_part = (
        kappa_sq
        + horiz_cond * (h_rowp + h_rowm + h_colp + h_colm)
        + vert_cond * (v_above + v_below)
    )
    c_below, c_above = vert_cond * v_below, vert_cond * v_above
    c_rowm, c_rowp = horiz_cond * h_rowm, horiz_cond * h_rowp
    c_colm, c_colp = horiz_cond * h_colm, horiz_cond * h_colp

    def kcombine(u, below, above, rowm, rowp):
        flux = (
            c_rowp * rowp
            + c_rowm * rowm
            + c_colp * column_up(u)
            + c_colm * column_down(u)
            + c_above * above
            + c_below * below
        )
        return diag_part * u - flux

    def kapply(u):
        below, above = neighbours(u, "depth", 1)
        rowm, rowp = neighbours(u, "tile", 2)
        return kcombine(u, below, above, rowm, rowp)

    width = 2 * samples

    def line_solve(resid_in):
        back, message = pl.pallas_call(
            sweep_kernel,
            out_shape=(
                jax.ShapeDtypeStruct(resid_in.shape, f32),
                jax.ShapeDtypeStruct((2, samples) + block_shape[1:], f32),
            ),
        )(resid_in, line_lower, line_pivot)
        messages = gather_depth(message.reshape((width,) + block_shape[1:]))
        count = messages.shape[0]
        enter_all, top_all = pl.pallas_call(
            scan_kernel,
            out_shape=(
                jax.ShapeDtypeStruct((count, samples) + block_shape[1:], f32),
                jax.ShapeDtypeStruct((count, samples) + block_shape[1:], f32),
            ),
        )(messages, consts_all)
        mine = lax.axis_index("depth")
        enter = lax.dynamic_index_in_dim(enter_all, mine, 0, keepdims=False)
        top = lax.dynamic_index_in_dim(top_all, mine, 0, keepdims=False)
        result = back + enter[:, None] * h_field[None] + top[:, None] * gain_up[None]
        return result

    k_joint = kcombine(
        joint[:lead], j_below[:lead], j_above[:lead], j_rowm[:lead], j_rowp[:lead]
    )
    right_side = k_joint[:samples] + obs_rhs
    basis_flat = deflation.reshape(vectors, cell_count)
    kbasis = k_joint[samples:]
    abasis_flat = (kapply(kbasis) + obs_diag * deflation).reshape(vectors, cell_count)
    gram_part = cells_dot(basis_flat, abasis_flat)
    proj_part = cells_dot(basis_flat, right_side.reshape(samples, cell_count))
    upper_row, upper_col = jnp.triu_indices(vectors)
    gram_half = (0.5 * (gram_part + gram_part.T))[upper_row, upper_col]
    first = all_sum(jnp.concatenate([gram_half, proj_part.reshape(-1)]))
    tri = upper_row.size
    gram_matrix = jnp.zeros((vectors, vectors), f32).at[upper_row, upper_col].set(first[:tri])
    gram_matrix = gram_matrix.at[upper_col, upper_row].set(first[:tri])
    proj_rhs = first[tri:].reshape(vectors, samples)
    chol_factor = jnp.linalg.cholesky(gram_matrix)

    def coarse(terms):
        return jax.scipy.linalg.cho_solve((chol_factor, True), terms)

    def expand(rows_flat, coarse_coef):
        return jnp.dot(coarse_coef.T, rows_flat, precision=PRECISE).reshape(prior_noise.shape)

    def inner_sum(left_side, right_part):
        return jnp.sum(left_side * right_part, axis=(1, 2, 3))

    def project(field_in):
        return cells_dot(abasis_flat, field_in.reshape(samples, cell_count))

    coarse_coef = coarse(proj_rhs)
    solution = expand(basis_flat, coarse_coef)
    residual = right_side - expand(abasis_flat, coarse_coef)

    precond = line_solve(residual)
    k_precond = kapply(precond)
    sums = all_sum(
        jnp.concatenate(
            [
                inner_sum(residual, precond),
                inner_sum(k_precond, k_precond) + inner_sum(obs_diag * precond, precond),
                project(precond).reshape(-1),
            ]
        )
    )
    rz_now, pap = sums[:samples], sums[samples : 2 * samples]
    proj_now = sums[2 * samples :].reshape(vectors, samples)
    a_precond = kapply(k_precond) + obs_diag * precond
    coarse_dir = coarse(proj_now)
    direction = precond - expand(basis_flat, coarse_dir)
    image_dir = a_precond - expand(abasis_flat, coarse_dir)
    curve_val = pap - jnp.sum(coarse_dir * proj_now, 0)
    step_field = (rz_now / curve_val)[:, None, None, None]
    solution = solution + step_field * direction
    residual = residual - step_field * image_dir

    precond = line_solve(residual)
    k_precond = kapply(precond)
    sums = all_sum(
        jnp.concatenate(
            [
                inner_sum(residual, precond),
                inner_sum(k_precond, k_precond) + inner_sum(obs_diag * precond, precond),
                inner_sum(image_dir, precond),
                project(precond).reshape(-1),
                project(direction).reshape(-1),
            ]
        )
    )
    rz_next, pap, cross = sums[:samples], sums[samples : 2 * samples], sums[2 * samples : 3 * samples]
    rest = sums[3 * samples :]
    proj_now = rest[: vectors * samples].reshape(vectors, samples)
    proj_old = rest[vectors * samples :].reshape(vectors, samples)
    a_precond = kapply(k_precond) + obs_diag * precond
    coarse_dir = coarse(proj_now)
    beta = rz_next / rz_now
    beta_ratio = beta[:, None, None, None]
    direction = precond + beta_ratio * direction - expand(basis_flat, coarse_dir)
    image_dir = a_precond + beta_ratio * image_dir - expand(abasis_flat, coarse_dir)
    curve_val = (
        pap
        + 2.0 * beta * cross
        + beta * beta * curve_val
        - jnp.sum(coarse_dir * proj_now, 0)
        - 2.0 * beta * jnp.sum(coarse_dir * proj_old, 0)
    )
    step_field = (rz_next / curve_val)[:, None, None, None]
    solution = solution + step_field * direction
    residual = residual - step_field * image_dir
    return (solution, residual)


def solution(mesh):
    return jax.shard_map(
        per_device,
        mesh=mesh,
        in_specs=(
            P(None, "depth", "tile", None),
            P("depth", "tile", None),
            P("depth", "tile", None),
            P("depth", "tile", None),
            P("depth", "tile", None),
            P("depth", "tile", None),
            P(None, "depth", "tile", None),
            P(None, "tile", "depth", None, None),
            P("tile", "depth", None, None),
            P("tile", "depth", None, None),
            P("tile", "depth", None),
        ),
        out_specs=(P(None, "depth", "tile", None), P(None, "depth", "tile", None)),
        check_vma=False,
    )
```

```python
import jax
import jax.numpy as jnp
from jax import lax
from jax.experimental import pallas as pl
from jax.sharding import PartitionSpec as P

ITERS = 2


PRECISE = lax.Precision.HIGHEST


def all_sum(x):
    count = lax.axis_size("tile") * lax.axis_size("depth")
    spread = jnp.broadcast_to(x[None], (count,) + x.shape)
    return jnp.sum(lax.all_to_all(spread, ("tile", "depth"), 0, 0, tiled=False), 0)


def gather_depth(x):
    count = lax.axis_size("depth")
    spread = jnp.broadcast_to(x[None], (count,) + x.shape)
    return lax.all_to_all(spread, "depth", 0, 0, tiled=False)


def neighbours(array, axis, dim):
    count, length = lax.axis_size(axis), array.shape[dim]
    up = [(i, i + 1) for i in range(count - 1)]
    down = [(i + 1, i) for i in range(count - 1)]
    last = lax.slice_in_dim(array, length - 1, length, axis=dim)
    first = lax.slice_in_dim(array, 0, 1, axis=dim)
    before = lax.ppermute(last, axis, up)
    after = lax.ppermute(first, axis, down)
    lower = jnp.concatenate([before, lax.slice_in_dim(array, 0, length - 1, axis=dim)], dim)
    upper = jnp.concatenate([lax.slice_in_dim(array, 1, length, axis=dim), after], dim)
    return lower, upper


def column_up(vector_in):
    return jnp.concatenate([vector_in[..., 1:], jnp.zeros_like(vector_in[..., :1])], -1)


def column_down(vector_in):
    return jnp.concatenate([jnp.zeros_like(vector_in[..., :1]), vector_in[..., :-1]], -1)


def cells_dot(left_rows, right_rows):
    return lax.dot_general(left_rows, right_rows, (((1,), (1,)), ((), ())), precision=PRECISE)


def prep_kernel(low_ref, piv_ref, gd_ref, gu_ref, h_ref, c_ref):
    layers = low_ref.shape[0]
    g = -low_ref[0]
    gd_ref[0] = g
    for i in range(1, layers):
        g = -low_ref[i] * g
        gd_ref[i] = g
    u = jnp.ones_like(g)
    gu_ref[layers - 1] = u
    for i in range(layers - 2, -1, -1):
        u = -low_ref[i + 1] * u
        gu_ref[i] = u
    z = gd_ref[layers - 1] / piv_ref[layers - 1]
    h_ref[layers - 1] = z
    for i in range(layers - 2, -1, -1):
        z = gd_ref[i] / piv_ref[i] - low_ref[i + 1] * z
        h_ref[i] = z
    c_ref[0] = gd_ref[layers - 1]
    c_ref[1] = -low_ref[0] * z
    c_ref[2] = -low_ref[0] * u


def sweep_kernel(r_ref, low_ref, piv_ref, bw_ref, msg_ref):
    layers = r_ref.shape[1]
    y = r_ref[:, 0]
    bw_ref[:, 0] = y / piv_ref[0][None]
    for i in range(1, layers):
        y = r_ref[:, i] - low_ref[i][None] * y
        bw_ref[:, i] = y / piv_ref[i][None]
    msg_ref[0] = y
    z = bw_ref[:, layers - 1]
    for i in range(layers - 2, -1, -1):
        z = bw_ref[:, i] - low_ref[i + 1][None] * z
        bw_ref[:, i] = z
    msg_ref[1] = -low_ref[0][None] * z


def scan_kernel(msg_ref, c_ref, e_ref, t_ref):
    count, samples = msg_ref.shape[0], e_ref.shape[1]
    base = 0
    e = jnp.zeros(e_ref.shape[1:], jnp.float32)
    e_ref[0] = e
    for k in range(count - 1):
        e = msg_ref[k, 0:samples] + c_ref[k, base][None] * e
        e_ref[k + 1] = e
    t = jnp.zeros_like(e)
    t_ref[count - 1] = t
    for k in range(count - 1, 0, -1):
        offset = msg_ref[k, samples : 2 * samples] + c_ref[k, base + 1][None] * e_ref[k]
        t = offset + c_ref[k, base + 2][None] * t
        t_ref[k - 1] = t


def per_device(
    prior_noise,
    kappa_sq,
    horiz_cond,
    vert_cond,
    line_lower,
    line_pivot,
    deflation,
    obs_value,
    obs_weight,
    obs_cell,
    obs_count,
):
    samples = prior_noise.shape[0]
    vectors = deflation.shape[0]
    block_shape = prior_noise.shape[1:]
    layers = block_shape[0]
    cell_count = kappa_sq.size
    f32 = jnp.float32
    field = jax.ShapeDtypeStruct(block_shape, f32)
    gain_down, gain_up, h_field, consts = pl.pallas_call(
        prep_kernel,
        out_shape=(field, field, field, jax.ShapeDtypeStruct((3,) + block_shape[1:], f32)),
    )(line_lower, line_pivot)
    count = lax.axis_size("depth")
    value_rows = jnp.transpose(obs_value[:, 0, 0], (1, 0, 2)).reshape(count, -1)
    obs_rows = jnp.concatenate([value_rows, obs_weight[0, 0]], 1)
    lane = consts.shape[-1]
    obs_width = obs_rows.shape[1]
    obs_rows = jnp.pad(obs_rows, ((0, 0), (0, -obs_width % lane))).reshape(count, -1, lane)
    const_rows = jnp.broadcast_to(
        consts.reshape(1, -1, lane), (count, consts.size // lane, lane)
    )
    got = lax.all_to_all(
        jnp.concatenate([const_rows, obs_rows], 1), "depth", 0, 0, tiled=False
    )
    consts_all = got[:, : consts.size // lane].reshape((count,) + consts.shape)
    obs_got = got[:, consts.size // lane :].reshape(count, -1)[:, :obs_width]
    slots = obs_width // (samples + 1)
    got_value = jnp.transpose(obs_got[:, : samples * slots].reshape(count, samples, slots), (1, 0, 2))
    got_weight = obs_got[:, samples * slots :]
    slot_index = lax.broadcasted_iota(jnp.int32, obs_cell.shape[2:], 1)
    live_slot = (slot_index < obs_count[0, 0][:, None]).astype(f32).reshape(-1)
    weights = got_weight.reshape(-1) * live_slot
    targets = obs_cell.reshape(-1)
    planes, cols = cell_count // block_shape[2], block_shape[2]
    plane_hot = (
        lax.broadcasted_iota(jnp.int32, (planes, targets.size), 0) == (targets // cols)[None]
    ).astype(f32)
    col_hot = (
        lax.broadcasted_iota(jnp.int32, (targets.size, cols), 1) == (targets % cols)[:, None]
    ).astype(f32)
    slot_terms = jnp.concatenate([got_value.reshape(samples, -1) * weights[None], weights[None]], 0)
    placed = jnp.einsum(
        "po,joc->jpc", plane_hot, slot_terms[:, :, None] * col_hot[None], precision=PRECISE
    )
    obs_rhs = placed[:samples].reshape(prior_noise.shape)
    obs_diag = placed[samples].reshape(block_shape)

    joint = jnp.concatenate(
        [prior_noise, deflation, horiz_cond[None], vert_cond[None]], 0
    )
    j_below, j_above = neighbours(joint, "depth", 1)
    j_rowm, j_rowp = neighbours(joint, "tile", 2)
    lead = samples + vectors
    v_below, v_above = j_below[lead + 1], j_above[lead + 1]
    h_rowm, h_rowp = j_rowm[lead], j_rowp[lead]
    h_colp, h_colm = column_up(horiz_cond), column_down(horiz_cond)
    diag_part = (
        kappa_sq
        + horiz_cond * (h_rowp + h_rowm + h_colp + h_colm)
        + vert_cond * (v_above + v_below)
    )
    c_below, c_above = vert_cond * v_below, vert_cond * v_above
    c_rowm, c_rowp = horiz_cond * h_rowm, horiz_cond * h_rowp
    c_colm, c_colp = horiz_cond * h_colm, horiz_cond * h_colp

    def kcombine(u, below, above, rowm, rowp):
        flux = (
            c_rowp * rowp
            + c_rowm * rowm
            + c_colp * column_up(u)
            + c_colm * column_down(u)
            + c_above * above
            + c_below * below
        )
        return diag_part * u - flux

    def kapply(u):
        below, above = neighbours(u, "depth", 1)
        rowm, rowp = neighbours(u, "tile", 2)
        return kcombine(u, below, above, rowm, rowp)

    width = 2 * samples

    def line_solve(resid_in):
        back, message = pl.pallas_call(
            sweep_kernel,
            out_shape=(
                jax.ShapeDtypeStruct(resid_in.shape, f32),
                jax.ShapeDtypeStruct((2, samples) + block_shape[1:], f32),
            ),
        )(resid_in, line_lower, line_pivot)
        messages = gather_depth(message.reshape((width,) + block_shape[1:]))
        count = messages.shape[0]
        enter_all, top_all = pl.pallas_call(
            scan_kernel,
            out_shape=(
                jax.ShapeDtypeStruct((count, samples) + block_shape[1:], f32),
                jax.ShapeDtypeStruct((count, samples) + block_shape[1:], f32),
            ),
        )(messages, consts_all)
        mine = lax.axis_index("depth")
        enter = lax.dynamic_index_in_dim(enter_all, mine, 0, keepdims=False)
        top = lax.dynamic_index_in_dim(top_all, mine, 0, keepdims=False)
        result = back + enter[:, None] * h_field[None] + top[:, None] * gain_up[None]
        return result

    k_joint = kcombine(
        joint[:lead], j_below[:lead], j_above[:lead], j_rowm[:lead], j_rowp[:lead]
    )
    right_side = k_joint[:samples] + obs_rhs
    basis_flat = deflation.reshape(vectors, cell_count)
    kbasis = k_joint[samples:]
    abasis_flat = (kapply(kbasis) + obs_diag * deflation).reshape(vectors, cell_count)
    gram_part = cells_dot(basis_flat, abasis_flat)
    proj_part = cells_dot(basis_flat, right_side.reshape(samples, cell_count))
    first = all_sum(jnp.concatenate([gram_part.reshape(-1), proj_part.reshape(-1)]))
    gram_total = first[: vectors * vectors].reshape(vectors, vectors)
    proj_rhs = first[vectors * vectors :].reshape(vectors, samples)
    gram_matrix = 0.5 * (gram_total + gram_total.T)
    chol_factor = jnp.linalg.cholesky(gram_matrix)

    def coarse(terms):
        return jax.scipy.linalg.cho_solve((chol_factor, True), terms)

    def expand(rows_flat, coarse_coef):
        return jnp.dot(coarse_coef.T, rows_flat, precision=PRECISE).reshape(prior_noise.shape)

    def inner_sum(left_side, right_part):
        return jnp.sum(left_side * right_part, axis=(1, 2, 3))

    def project(field_in):
        return cells_dot(abasis_flat, field_in.reshape(samples, cell_count))

    coarse_coef = coarse(proj_rhs)
    solution = expand(basis_flat, coarse_coef)
    residual = right_side - expand(abasis_flat, coarse_coef)

    precond = line_solve(residual)
    k_precond = kapply(precond)
    sums = all_sum(
        jnp.concatenate(
            [
                inner_sum(residual, precond),
                inner_sum(k_precond, k_precond) + inner_sum(obs_diag * precond, precond),
                project(precond).reshape(-1),
            ]
        )
    )
    rz_now, pap = sums[:samples], sums[samples : 2 * samples]
    proj_now = sums[2 * samples :].reshape(vectors, samples)
    a_precond = kapply(k_precond) + obs_diag * precond
    coarse_dir = coarse(proj_now)
    direction = precond - expand(basis_flat, coarse_dir)
    image_dir = a_precond - expand(abasis_flat, coarse_dir)
    curve_val = pap - jnp.sum(coarse_dir * proj_now, 0)
    step_field = (rz_now / curve_val)[:, None, None, None]
    solution = solution + step_field * direction
    residual = residual - step_field * image_dir

    precond = line_solve(residual)
    k_precond = kapply(precond)
    sums = all_sum(
        jnp.concatenate(
            [
                inner_sum(residual, precond),
                inner_sum(k_precond, k_precond) + inner_sum(obs_diag * precond, precond),
                inner_sum(image_dir, precond),
                project(precond).reshape(-1),
                project(direction).reshape(-1),
            ]
        )
    )
    rz_next, pap, cross = sums[:samples], sums[samples : 2 * samples], sums[2 * samples : 3 * samples]
    rest = sums[3 * samples :]
    proj_now = rest[: vectors * samples].reshape(vectors, samples)
    proj_old = rest[vectors * samples :].reshape(vectors, samples)
    a_precond = kapply(k_precond) + obs_diag * precond
    coarse_dir = coarse(proj_now)
    beta = rz_next / rz_now
    beta_ratio = beta[:, None, None, None]
    direction = precond + beta_ratio * direction - expand(basis_flat, coarse_dir)
    image_dir = a_precond + beta_ratio * image_dir - expand(abasis_flat, coarse_dir)
    curve_val = (
        pap
        + 2.0 * beta * cross
        + beta * beta * curve_val
        - jnp.sum(coarse_dir * proj_now, 0)
        - 2.0 * beta * jnp.sum(coarse_dir * proj_old, 0)
    )
    step_field = (rz_next / curve_val)[:, None, None, None]
    solution = solution + step_field * direction
    residual = residual - step_field * image_dir
    return (solution, residual)


def solution(mesh):
    return jax.shard_map(
        per_device,
        mesh=mesh,
        in_specs=(
            P(None, "depth", "tile", None),
            P("depth", "tile", None),
            P("depth", "tile", None),
            P("depth", "tile", None),
            P("depth", "tile", None),
            P("depth", "tile", None),
            P(None, "depth", "tile", None),
            P(None, "tile", "depth", None, None),
            P("tile", "depth", None, None),
            P("tile", "depth", None, None),
            P("tile", "depth", None),
        ),
        out_specs=(P(None, "depth", "tile", None), P(None, "depth", "tile", None)),
        check_vma=False,
    )
```

```python
import jax
import jax.numpy as jnp
from jax import lax
from jax.experimental import pallas as pl
from jax.sharding import PartitionSpec as P

ITERS = 2


PRECISE = lax.Precision.HIGHEST


def all_sum(x):
    count = lax.axis_size("tile") * lax.axis_size("depth")
    size = x.shape[0]
    rows = jnp.pad(x, (0, -size % 128)).reshape(-1, 128)
    spread = jnp.broadcast_to(rows[None], (count,) + rows.shape)
    total = jnp.sum(lax.all_to_all(spread, ("tile", "depth"), 0, 0, tiled=False), 0)
    return total.reshape(-1)[:size]


def gather_depth(x):
    count = lax.axis_size("depth")
    spread = jnp.broadcast_to(x[None], (count,) + x.shape)
    return lax.all_to_all(spread, "depth", 0, 0, tiled=False)


def neighbours(array, axis, dim):
    count, length = lax.axis_size(axis), array.shape[dim]
    up = [(i, i + 1) for i in range(count - 1)]
    down = [(i + 1, i) for i in range(count - 1)]
    last = lax.slice_in_dim(array, length - 1, length, axis=dim)
    first = lax.slice_in_dim(array, 0, 1, axis=dim)
    before = lax.ppermute(last, axis, up)
    after = lax.ppermute(first, axis, down)
    lower = jnp.concatenate([before, lax.slice_in_dim(array, 0, length - 1, axis=dim)], dim)
    upper = jnp.concatenate([lax.slice_in_dim(array, 1, length, axis=dim), after], dim)
    return lower, upper


def column_up(vector_in):
    return jnp.concatenate([vector_in[..., 1:], jnp.zeros_like(vector_in[..., :1])], -1)


def column_down(vector_in):
    return jnp.concatenate([jnp.zeros_like(vector_in[..., :1]), vector_in[..., :-1]], -1)


def cells_dot(left_rows, right_rows):
    return lax.dot_general(left_rows, right_rows, (((1,), (1,)), ((), ())), precision=PRECISE)


def prep_kernel(low_ref, piv_ref, gd_ref, gu_ref, h_ref, c_ref):
    layers = low_ref.shape[0]
    g = -low_ref[0]
    gd_ref[0] = g
    for i in range(1, layers):
        g = -low_ref[i] * g
        gd_ref[i] = g
    u = jnp.ones_like(g)
    gu_ref[layers - 1] = u
    for i in range(layers - 2, -1, -1):
        u = -low_ref[i + 1] * u
        gu_ref[i] = u
    z = gd_ref[layers - 1] / piv_ref[layers - 1]
    h_ref[layers - 1] = z
    for i in range(layers - 2, -1, -1):
        z = gd_ref[i] / piv_ref[i] - low_ref[i + 1] * z
        h_ref[i] = z
    c_ref[0] = gd_ref[layers - 1]
    c_ref[1] = -low_ref[0] * z
    c_ref[2] = -low_ref[0] * u


def sweep_kernel(r_ref, low_ref, piv_ref, bw_ref, msg_ref):
    layers = r_ref.shape[1]
    y = r_ref[:, 0]
    bw_ref[:, 0] = y / piv_ref[0][None]
    for i in range(1, layers):
        y = r_ref[:, i] - low_ref[i][None] * y
        bw_ref[:, i] = y / piv_ref[i][None]
    msg_ref[0] = y
    z = bw_ref[:, layers - 1]
    for i in range(layers - 2, -1, -1):
        z = bw_ref[:, i] - low_ref[i + 1][None] * z
        bw_ref[:, i] = z
    msg_ref[1] = -low_ref[0][None] * z


def scan_kernel(msg_ref, c_ref, e_ref, t_ref):
    count, samples = msg_ref.shape[0], e_ref.shape[1]
    base = 0
    e = jnp.zeros(e_ref.shape[1:], jnp.float32)
    e_ref[0] = e
    for k in range(count - 1):
        e = msg_ref[k, 0:samples] + c_ref[k, base][None] * e
        e_ref[k + 1] = e
    t = jnp.zeros_like(e)
    t_ref[count - 1] = t
    for k in range(count - 1, 0, -1):
        offset = msg_ref[k, samples : 2 * samples] + c_ref[k, base + 1][None] * e_ref[k]
        t = offset + c_ref[k, base + 2][None] * t
        t_ref[k - 1] = t


def per_device(
    prior_noise,
    kappa_sq,
    horiz_cond,
    vert_cond,
    line_lower,
    line_pivot,
    deflation,
    obs_value,
    obs_weight,
    obs_cell,
    obs_count,
):
    samples = prior_noise.shape[0]
    vectors = deflation.shape[0]
    block_shape = prior_noise.shape[1:]
    layers = block_shape[0]
    cell_count = kappa_sq.size
    f32 = jnp.float32
    field = jax.ShapeDtypeStruct(block_shape, f32)
    gain_down, gain_up, h_field, consts = pl.pallas_call(
        prep_kernel,
        out_shape=(field, field, field, jax.ShapeDtypeStruct((3,) + block_shape[1:], f32)),
    )(line_lower, line_pivot)
    count = lax.axis_size("depth")
    value_rows = jnp.transpose(obs_value[:, 0, 0], (1, 0, 2)).reshape(count, -1)
    obs_rows = jnp.concatenate([value_rows, obs_weight[0, 0]], 1)
    lane = consts.shape[-1]
    obs_width = obs_rows.shape[1]
    obs_rows = jnp.pad(obs_rows, ((0, 0), (0, -obs_width % lane))).reshape(count, -1, lane)
    const_rows = jnp.broadcast_to(
        consts.reshape(1, -1, lane), (count, consts.size // lane, lane)
    )
    got = lax.all_to_all(
        jnp.concatenate([const_rows, obs_rows], 1), "depth", 0, 0, tiled=False
    )
    consts_all = got[:, : consts.size // lane].reshape((count,) + consts.shape)
    obs_got = got[:, consts.size // lane :].reshape(count, -1)[:, :obs_width]
    slots = obs_width // (samples + 1)
    got_value = jnp.transpose(obs_got[:, : samples * slots].reshape(count, samples, slots), (1, 0, 2))
    got_weight = obs_got[:, samples * slots :]
    slot_index = lax.broadcasted_iota(jnp.int32, obs_cell.shape[2:], 1)
    live_slot = (slot_index < obs_count[0, 0][:, None]).astype(f32).reshape(-1)
    weights = got_weight.reshape(-1) * live_slot
    targets = obs_cell.reshape(-1)
    planes, cols = cell_count // block_shape[2], block_shape[2]
    plane_hot = (
        lax.broadcasted_iota(jnp.int32, (planes, targets.size), 0) == (targets // cols)[None]
    ).astype(f32)
    col_hot = (
        lax.broadcasted_iota(jnp.int32, (targets.size, cols), 1) == (targets % cols)[:, None]
    ).astype(f32)
    slot_terms = jnp.concatenate([got_value.reshape(samples, -1) * weights[None], weights[None]], 0)
    placed = jnp.einsum(
        "po,joc->jpc", plane_hot, slot_terms[:, :, None] * col_hot[None], precision=PRECISE
    )
    obs_rhs = placed[:samples].reshape(prior_noise.shape)
    obs_diag = placed[samples].reshape(block_shape)

    joint = jnp.concatenate(
        [prior_noise, deflation, horiz_cond[None], vert_cond[None]], 0
    )
    j_below, j_above = neighbours(joint, "depth", 1)
    j_rowm, j_rowp = neighbours(joint, "tile", 2)
    lead = samples + vectors
    v_below, v_above = j_below[lead + 1], j_above[lead + 1]
    h_rowm, h_rowp = j_rowm[lead], j_rowp[lead]
    h_colp, h_colm = column_up(horiz_cond), column_down(horiz_cond)
    diag_part = (
        kappa_sq
        + horiz_cond * (h_rowp + h_rowm + h_colp + h_colm)
        + vert_cond * (v_above + v_below)
    )
    c_below, c_above = vert_cond * v_below, vert_cond * v_above
    c_rowm, c_rowp = horiz_cond * h_rowm, horiz_cond * h_rowp
    c_colm, c_colp = horiz_cond * h_colm, horiz_cond * h_colp

    def kcombine(u, below, above, rowm, rowp):
        flux = (
            c_rowp * rowp
            + c_rowm * rowm
            + c_colp * column_up(u)
            + c_colm * column_down(u)
            + c_above * above
            + c_below * below
        )
        return diag_part * u - flux

    def kapply(u):
        below, above = neighbours(u, "depth", 1)
        rowm, rowp = neighbours(u, "tile", 2)
        return kcombine(u, below, above, rowm, rowp)

    width = 2 * samples

    def line_solve(resid_in):
        back, message = pl.pallas_call(
            sweep_kernel,
            out_shape=(
                jax.ShapeDtypeStruct(resid_in.shape, f32),
                jax.ShapeDtypeStruct((2, samples) + block_shape[1:], f32),
            ),
        )(resid_in, line_lower, line_pivot)
        messages = gather_depth(message.reshape((width,) + block_shape[1:]))
        count = messages.shape[0]
        enter_all, top_all = pl.pallas_call(
            scan_kernel,
            out_shape=(
                jax.ShapeDtypeStruct((count, samples) + block_shape[1:], f32),
                jax.ShapeDtypeStruct((count, samples) + block_shape[1:], f32),
            ),
        )(messages, consts_all)
        mine = lax.axis_index("depth")
        enter = lax.dynamic_index_in_dim(enter_all, mine, 0, keepdims=False)
        top = lax.dynamic_index_in_dim(top_all, mine, 0, keepdims=False)
        result = back + enter[:, None] * h_field[None] + top[:, None] * gain_up[None]
        return result

    k_joint = kcombine(
        joint[:lead], j_below[:lead], j_above[:lead], j_rowm[:lead], j_rowp[:lead]
    )
    right_side = k_joint[:samples] + obs_rhs
    basis_flat = deflation.reshape(vectors, cell_count)
    kbasis = k_joint[samples:]
    abasis_flat = (kapply(kbasis) + obs_diag * deflation).reshape(vectors, cell_count)
    gram_part = cells_dot(basis_flat, abasis_flat)
    proj_part = cells_dot(basis_flat, right_side.reshape(samples, cell_count))
    first = all_sum(jnp.concatenate([gram_part.reshape(-1), proj_part.reshape(-1)]))
    gram_total = first[: vectors * vectors].reshape(vectors, vectors)
    proj_rhs = first[vectors * vectors :].reshape(vectors, samples)
    gram_matrix = 0.5 * (gram_total + gram_total.T)
    chol_factor = jnp.linalg.cholesky(gram_matrix)

    def coarse(terms):
        return jax.scipy.linalg.cho_solve((chol_factor, True), terms)

    def expand(rows_flat, coarse_coef):
        return jnp.dot(coarse_coef.T, rows_flat, precision=PRECISE).reshape(prior_noise.shape)

    def inner_sum(left_side, right_part):
        return jnp.sum(left_side * right_part, axis=(1, 2, 3))

    def project(field_in):
        return cells_dot(abasis_flat, field_in.reshape(samples, cell_count))

    coarse_coef = coarse(proj_rhs)
    solution = expand(basis_flat, coarse_coef)
    residual = right_side - expand(abasis_flat, coarse_coef)

    precond = line_solve(residual)
    k_precond = kapply(precond)
    sums = all_sum(
        jnp.concatenate(
            [
                inner_sum(residual, precond),
                inner_sum(k_precond, k_precond) + inner_sum(obs_diag * precond, precond),
                project(precond).reshape(-1),
            ]
        )
    )
    rz_now, pap = sums[:samples], sums[samples : 2 * samples]
    proj_now = sums[2 * samples :].reshape(vectors, samples)
    a_precond = kapply(k_precond) + obs_diag * precond
    coarse_dir = coarse(proj_now)
    direction = precond - expand(basis_flat, coarse_dir)
    image_dir = a_precond - expand(abasis_flat, coarse_dir)
    curve_val = pap - jnp.sum(coarse_dir * proj_now, 0)
    step_field = (rz_now / curve_val)[:, None, None, None]
    solution = solution + step_field * direction
    residual = residual - step_field * image_dir

    precond = line_solve(residual)
    k_precond = kapply(precond)
    sums = all_sum(
        jnp.concatenate(
            [
                inner_sum(residual, precond),
                inner_sum(k_precond, k_precond) + inner_sum(obs_diag * precond, precond),
                inner_sum(image_dir, precond),
                project(precond).reshape(-1),
                project(direction).reshape(-1),
            ]
        )
    )
    rz_next, pap, cross = sums[:samples], sums[samples : 2 * samples], sums[2 * samples : 3 * samples]
    rest = sums[3 * samples :]
    proj_now = rest[: vectors * samples].reshape(vectors, samples)
    proj_old = rest[vectors * samples :].reshape(vectors, samples)
    a_precond = kapply(k_precond) + obs_diag * precond
    coarse_dir = coarse(proj_now)
    beta = rz_next / rz_now
    beta_ratio = beta[:, None, None, None]
    direction = precond + beta_ratio * direction - expand(basis_flat, coarse_dir)
    image_dir = a_precond + beta_ratio * image_dir - expand(abasis_flat, coarse_dir)
    curve_val = (
        pap
        + 2.0 * beta * cross
        + beta * beta * curve_val
        - jnp.sum(coarse_dir * proj_now, 0)
        - 2.0 * beta * jnp.sum(coarse_dir * proj_old, 0)
    )
    step_field = (rz_next / curve_val)[:, None, None, None]
    solution = solution + step_field * direction
    residual = residual - step_field * image_dir
    return (solution, residual)


def solution(mesh):
    return jax.shard_map(
        per_device,
        mesh=mesh,
        in_specs=(
            P(None, "depth", "tile", None),
            P("depth", "tile", None),
            P("depth", "tile", None),
            P("depth", "tile", None),
            P("depth", "tile", None),
            P("depth", "tile", None),
            P(None, "depth", "tile", None),
            P(None, "tile", "depth", None, None),
            P("tile", "depth", None, None),
            P("tile", "depth", None, None),
            P("tile", "depth", None),
        ),
        out_specs=(P(None, "depth", "tile", None), P(None, "depth", "tile", None)),
        check_vma=False,
    )
```

```python
import jax
import jax.numpy as jnp
from jax import lax
from jax.experimental import pallas as pl
from jax.experimental.pallas import tpu as pltpu
from jax.sharding import PartitionSpec as P

ITERS = 2


PRECISE = lax.Precision.HIGHEST


def all_sum(x):
    count = lax.axis_size("tile") * lax.axis_size("depth")
    spread = jnp.broadcast_to(x[None], (count,) + x.shape)
    return jnp.sum(lax.all_to_all(spread, ("tile", "depth"), 0, 0, tiled=False), 0)


def gather_depth(x):
    count = lax.axis_size("depth")
    spread = jnp.broadcast_to(x[None], (count,) + x.shape)
    return lax.all_to_all(spread, "depth", 0, 0, tiled=False)


def neighbours(array, axis, dim):
    count, length = lax.axis_size(axis), array.shape[dim]
    up = [(i, i + 1) for i in range(count - 1)]
    down = [(i + 1, i) for i in range(count - 1)]
    last = lax.slice_in_dim(array, length - 1, length, axis=dim)
    first = lax.slice_in_dim(array, 0, 1, axis=dim)
    before = lax.ppermute(last, axis, up)
    after = lax.ppermute(first, axis, down)
    lower = jnp.concatenate([before, lax.slice_in_dim(array, 0, length - 1, axis=dim)], dim)
    upper = jnp.concatenate([lax.slice_in_dim(array, 1, length, axis=dim), after], dim)
    return lower, upper


def column_up(vector_in):
    return jnp.concatenate([vector_in[..., 1:], jnp.zeros_like(vector_in[..., :1])], -1)


def column_down(vector_in):
    return jnp.concatenate([jnp.zeros_like(vector_in[..., :1]), vector_in[..., :-1]], -1)


def cells_dot(left_rows, right_rows):
    return lax.dot_general(left_rows, right_rows, (((1,), (1,)), ((), ())), precision=PRECISE)


def prep_kernel(low_ref, piv_ref, gd_ref, gu_ref, h_ref, c_ref):
    layers = low_ref.shape[0]
    g = -low_ref[0]
    gd_ref[0] = g
    for i in range(1, layers):
        g = -low_ref[i] * g
        gd_ref[i] = g
    u = jnp.ones_like(g)
    gu_ref[layers - 1] = u
    for i in range(layers - 2, -1, -1):
        u = -low_ref[i + 1] * u
        gu_ref[i] = u
    z = gd_ref[layers - 1] / piv_ref[layers - 1]
    h_ref[layers - 1] = z
    for i in range(layers - 2, -1, -1):
        z = gd_ref[i] / piv_ref[i] - low_ref[i + 1] * z
        h_ref[i] = z
    c_ref[0] = gd_ref[layers - 1]
    c_ref[1] = -low_ref[0] * z
    c_ref[2] = -low_ref[0] * u


def sweep_kernel(r_ref, low_ref, piv_ref, bw_ref, msg_ref):
    layers = r_ref.shape[1]
    y = r_ref[:, 0]
    bw_ref[:, 0] = y / piv_ref[0][None]
    for i in range(1, layers):
        y = r_ref[:, i] - low_ref[i][None] * y
        bw_ref[:, i] = y / piv_ref[i][None]
    msg_ref[0] = y
    z = bw_ref[:, layers - 1]
    for i in range(layers - 2, -1, -1):
        z = bw_ref[:, i] - low_ref[i + 1][None] * z
        bw_ref[:, i] = z
    msg_ref[1] = -low_ref[0][None] * z


def scan_kernel(msg_ref, c_ref, sel_ref, e_out, t_out, e_all):
    count, samples = msg_ref.shape[0], e_out.shape[0]
    e = jnp.zeros(e_out.shape, jnp.float32)
    e_all[0] = e
    for k in range(count - 1):
        e = msg_ref[k, 0:samples] + c_ref[k, 0][None] * e
        e_all[k + 1] = e
    e_mine = jnp.zeros_like(e)
    for k in range(count):
        e_mine = e_mine + sel_ref[k][None] * e_all[k]
    e_out[...] = e_mine
    t = jnp.zeros_like(e)
    t_mine = sel_ref[count - 1][None] * t
    for k in range(count - 1, 0, -1):
        offset = msg_ref[k, samples : 2 * samples] + c_ref[k, 1][None] * e_all[k]
        t = offset + c_ref[k, 2][None] * t
        t_mine = t_mine + sel_ref[k - 1][None] * t
    t_out[...] = t_mine


def per_device(
    prior_noise,
    kappa_sq,
    horiz_cond,
    vert_cond,
    line_lower,
    line_pivot,
    deflation,
    obs_value,
    obs_weight,
    obs_cell,
    obs_count,
):
    samples = prior_noise.shape[0]
    vectors = deflation.shape[0]
    block_shape = prior_noise.shape[1:]
    layers = block_shape[0]
    cell_count = kappa_sq.size
    f32 = jnp.float32
    field = jax.ShapeDtypeStruct(block_shape, f32)
    gain_down, gain_up, h_field, consts = pl.pallas_call(
        prep_kernel,
        out_shape=(field, field, field, jax.ShapeDtypeStruct((3,) + block_shape[1:], f32)),
    )(line_lower, line_pivot)
    count = lax.axis_size("depth")
    value_rows = jnp.transpose(obs_value[:, 0, 0], (1, 0, 2)).reshape(count, -1)
    obs_rows = jnp.concatenate([value_rows, obs_weight[0, 0]], 1)
    lane = consts.shape[-1]
    obs_width = obs_rows.shape[1]
    obs_rows = jnp.pad(obs_rows, ((0, 0), (0, -obs_width % lane))).reshape(count, -1, lane)
    const_rows = jnp.broadcast_to(
        consts.reshape(1, -1, lane), (count, consts.size // lane, lane)
    )
    got = lax.all_to_all(
        jnp.concatenate([const_rows, obs_rows], 1), "depth", 0, 0, tiled=False
    )
    consts_all = got[:, : consts.size // lane].reshape((count,) + consts.shape)
    obs_got = got[:, consts.size // lane :].reshape(count, -1)[:, :obs_width]
    slots = obs_width // (samples + 1)
    got_value = jnp.transpose(obs_got[:, : samples * slots].reshape(count, samples, slots), (1, 0, 2))
    got_weight = obs_got[:, samples * slots :]
    slot_index = lax.broadcasted_iota(jnp.int32, obs_cell.shape[2:], 1)
    live_slot = (slot_index < obs_count[0, 0][:, None]).astype(f32).reshape(-1)
    weights = got_weight.reshape(-1) * live_slot
    targets = obs_cell.reshape(-1)
    planes, cols = cell_count // block_shape[2], block_shape[2]
    plane_hot = (
        lax.broadcasted_iota(jnp.int32, (planes, targets.size), 0) == (targets // cols)[None]
    ).astype(f32)
    col_hot = (
        lax.broadcasted_iota(jnp.int32, (targets.size, cols), 1) == (targets % cols)[:, None]
    ).astype(f32)
    slot_terms = jnp.concatenate([got_value.reshape(samples, -1) * weights[None], weights[None]], 0)
    placed = jnp.einsum(
        "po,joc->jpc", plane_hot, slot_terms[:, :, None] * col_hot[None], precision=PRECISE
    )
    obs_rhs = placed[:samples].reshape(prior_noise.shape)
    obs_diag = placed[samples].reshape(block_shape)

    joint = jnp.concatenate(
        [prior_noise, deflation, horiz_cond[None], vert_cond[None]], 0
    )
    j_below, j_above = neighbours(joint, "depth", 1)
    j_rowm, j_rowp = neighbours(joint, "tile", 2)
    lead = samples + vectors
    v_below, v_above = j_below[lead + 1], j_above[lead + 1]
    h_rowm, h_rowp = j_rowm[lead], j_rowp[lead]
    h_colp, h_colm = column_up(horiz_cond), column_down(horiz_cond)
    diag_part = (
        kappa_sq
        + horiz_cond * (h_rowp + h_rowm + h_colp + h_colm)
        + vert_cond * (v_above + v_below)
    )
    c_below, c_above = vert_cond * v_below, vert_cond * v_above
    c_rowm, c_rowp = horiz_cond * h_rowm, horiz_cond * h_rowp
    c_colm, c_colp = horiz_cond * h_colm, horiz_cond * h_colp

    def kcombine(u, below, above, rowm, rowp):
        flux = (
            c_rowp * rowp
            + c_rowm * rowm
            + c_colp * column_up(u)
            + c_colm * column_down(u)
            + c_above * above
            + c_below * below
        )
        return diag_part * u - flux

    def kapply(u):
        below, above = neighbours(u, "depth", 1)
        rowm, rowp = neighbours(u, "tile", 2)
        return kcombine(u, below, above, rowm, rowp)

    width = 2 * samples

    def line_solve(resid_in):
        back, message = pl.pallas_call(
            sweep_kernel,
            out_shape=(
                jax.ShapeDtypeStruct(resid_in.shape, f32),
                jax.ShapeDtypeStruct((2, samples) + block_shape[1:], f32),
            ),
        )(resid_in, line_lower, line_pivot)
        messages = gather_depth(message.reshape((width,) + block_shape[1:]))
        count = messages.shape[0]
        mine = lax.axis_index("depth")
        select = jnp.broadcast_to(
            (lax.iota(jnp.int32, count) == mine).astype(f32)[:, None, None],
            (count,) + block_shape[1:],
        )
        enter, top = pl.pallas_call(
            scan_kernel,
            out_shape=(
                jax.ShapeDtypeStruct((samples,) + block_shape[1:], f32),
                jax.ShapeDtypeStruct((samples,) + block_shape[1:], f32),
            ),
            scratch_shapes=[pltpu.VMEM((count, samples) + block_shape[1:], f32)],
        )(messages, consts_all, select)
        result = back + enter[:, None] * h_field[None] + top[:, None] * gain_up[None]
        return result

    k_joint = kcombine(
        joint[:lead], j_below[:lead], j_above[:lead], j_rowm[:lead], j_rowp[:lead]
    )
    right_side = k_joint[:samples] + obs_rhs
    basis_flat = deflation.reshape(vectors, cell_count)
    kbasis = k_joint[samples:]
    abasis_flat = (kapply(kbasis) + obs_diag * deflation).reshape(vectors, cell_count)
    gram_part = cells_dot(basis_flat, abasis_flat)
    proj_part = cells_dot(basis_flat, right_side.reshape(samples, cell_count))
    first = all_sum(jnp.concatenate([gram_part.reshape(-1), proj_part.reshape(-1)]))
    gram_total = first[: vectors * vectors].reshape(vectors, vectors)
    proj_rhs = first[vectors * vectors :].reshape(vectors, samples)
    gram_matrix = 0.5 * (gram_total + gram_total.T)
    chol_factor = jnp.linalg.cholesky(gram_matrix)

    def coarse(terms):
        return jax.scipy.linalg.cho_solve((chol_factor, True), terms)

    def expand(rows_flat, coarse_coef):
        return jnp.dot(coarse_coef.T, rows_flat, precision=PRECISE).reshape(prior_noise.shape)

    def inner_sum(left_side, right_part):
        return jnp.sum(left_side * right_part, axis=(1, 2, 3))

    def project(field_in):
        return cells_dot(abasis_flat, field_in.reshape(samples, cell_count))

    coarse_coef = coarse(proj_rhs)
    solution = expand(basis_flat, coarse_coef)
    residual = right_side - expand(abasis_flat, coarse_coef)

    precond = line_solve(residual)
    k_precond = kapply(precond)
    sums = all_sum(
        jnp.concatenate(
            [
                inner_sum(residual, precond),
                inner_sum(k_precond, k_precond) + inner_sum(obs_diag * precond, precond),
                project(precond).reshape(-1),
            ]
        )
    )
    rz_now, pap = sums[:samples], sums[samples : 2 * samples]
    proj_now = sums[2 * samples :].reshape(vectors, samples)
    a_precond = kapply(k_precond) + obs_diag * precond
    coarse_dir = coarse(proj_now)
    direction = precond - expand(basis_flat, coarse_dir)
    image_dir = a_precond - expand(abasis_flat, coarse_dir)
    curve_val = pap - jnp.sum(coarse_dir * proj_now, 0)
    step_field = (rz_now / curve_val)[:, None, None, None]
    solution = solution + step_field * direction
    residual = residual - step_field * image_dir

    precond = line_solve(residual)
    k_precond = kapply(precond)
    sums = all_sum(
        jnp.concatenate(
            [
                inner_sum(residual, precond),
                inner_sum(k_precond, k_precond) + inner_sum(obs_diag * precond, precond),
                inner_sum(image_dir, precond),
                project(precond).reshape(-1),
                project(direction).reshape(-1),
            ]
        )
    )
    rz_next, pap, cross = sums[:samples], sums[samples : 2 * samples], sums[2 * samples : 3 * samples]
    rest = sums[3 * samples :]
    proj_now = rest[: vectors * samples].reshape(vectors, samples)
    proj_old = rest[vectors * samples :].reshape(vectors, samples)
    a_precond = kapply(k_precond) + obs_diag * precond
    coarse_dir = coarse(proj_now)
    beta = rz_next / rz_now
    beta_ratio = beta[:, None, None, None]
    direction = precond + beta_ratio * direction - expand(basis_flat, coarse_dir)
    image_dir = a_precond + beta_ratio * image_dir - expand(abasis_flat, coarse_dir)
    curve_val = (
        pap
        + 2.0 * beta * cross
        + beta * beta * curve_val
        - jnp.sum(coarse_dir * proj_now, 0)
        - 2.0 * beta * jnp.sum(coarse_dir * proj_old, 0)
    )
    step_field = (rz_next / curve_val)[:, None, None, None]
    solution = solution + step_field * direction
    residual = residual - step_field * image_dir
    return (solution, residual)


def solution(mesh):
    return jax.shard_map(
        per_device,
        mesh=mesh,
        in_specs=(
            P(None, "depth", "tile", None),
            P("depth", "tile", None),
            P("depth", "tile", None),
            P("depth", "tile", None),
            P("depth", "tile", None),
            P("depth", "tile", None),
            P(None, "depth", "tile", None),
            P(None, "tile", "depth", None, None),
            P("tile", "depth", None, None),
            P("tile", "depth", None, None),
            P("tile", "depth", None),
        ),
        out_specs=(P(None, "depth", "tile", None), P(None, "depth", "tile", None)),
        check_vma=False,
    )
```

```python
import jax
import jax.numpy as jnp
from jax import lax
from jax.experimental import pallas as pl
from jax.experimental.pallas import tpu as pltpu
from jax.sharding import PartitionSpec as P

ITERS = 2


PRECISE = lax.Precision.HIGHEST


def all_sum(x):
    count = lax.axis_size("tile") * lax.axis_size("depth")
    spread = jnp.broadcast_to(x[None], (count,) + x.shape)
    return jnp.sum(lax.all_to_all(spread, ("tile", "depth"), 0, 0, tiled=False), 0)


def gather_depth(x):
    count = lax.axis_size("depth")
    spread = jnp.broadcast_to(x[None], (count,) + x.shape)
    return lax.all_to_all(spread, "depth", 0, 0, tiled=False)


def neighbours(array, axis, dim):
    count, length = lax.axis_size(axis), array.shape[dim]
    up = [(i, i + 1) for i in range(count - 1)]
    down = [(i + 1, i) for i in range(count - 1)]
    last = lax.slice_in_dim(array, length - 1, length, axis=dim)
    first = lax.slice_in_dim(array, 0, 1, axis=dim)
    before = lax.ppermute(last, axis, up)
    after = lax.ppermute(first, axis, down)
    lower = jnp.concatenate([before, lax.slice_in_dim(array, 0, length - 1, axis=dim)], dim)
    upper = jnp.concatenate([lax.slice_in_dim(array, 1, length, axis=dim), after], dim)
    return lower, upper


def column_up(vector_in):
    return jnp.concatenate([vector_in[..., 1:], jnp.zeros_like(vector_in[..., :1])], -1)


def column_down(vector_in):
    return jnp.concatenate([jnp.zeros_like(vector_in[..., :1]), vector_in[..., :-1]], -1)


def cells_dot(left_rows, right_rows):
    return lax.dot_general(left_rows, right_rows, (((1,), (1,)), ((), ())), precision=PRECISE)


def prep_kernel(low_ref, piv_ref, gd_ref, gu_ref, h_ref, c_ref):
    layers = low_ref.shape[0]
    g = -low_ref[0]
    gd_ref[0] = g
    for i in range(1, layers):
        g = -low_ref[i] * g
        gd_ref[i] = g
    u = jnp.ones_like(g)
    gu_ref[layers - 1] = u
    for i in range(layers - 2, -1, -1):
        u = -low_ref[i + 1] * u
        gu_ref[i] = u
    z = gd_ref[layers - 1] / piv_ref[layers - 1]
    h_ref[layers - 1] = z
    for i in range(layers - 2, -1, -1):
        z = gd_ref[i] / piv_ref[i] - low_ref[i + 1] * z
        h_ref[i] = z
    c_ref[0] = gd_ref[layers - 1]
    c_ref[1] = -low_ref[0] * z
    c_ref[2] = -low_ref[0] * u


def sweep_kernel(r_ref, low_ref, piv_ref, bw_ref, msg_ref):
    layers = r_ref.shape[1]
    y = r_ref[:, 0]
    bw_ref[:, 0] = y / piv_ref[0][None]
    for i in range(1, layers):
        y = r_ref[:, i] - low_ref[i][None] * y
        bw_ref[:, i] = y / piv_ref[i][None]
    msg_ref[0] = y
    z = bw_ref[:, layers - 1]
    for i in range(layers - 2, -1, -1):
        z = bw_ref[:, i] - low_ref[i + 1][None] * z
        bw_ref[:, i] = z
    msg_ref[1] = -low_ref[0][None] * z


def scan_kernel(msg_ref, c_ref, sel_ref, back_ref, h_ref, gu_ref, out_ref, e_all):
    count, samples = msg_ref.shape[0], out_ref.shape[0]
    e = jnp.zeros((samples,) + out_ref.shape[2:], jnp.float32)
    e_all[0] = e
    for k in range(count - 1):
        e = msg_ref[k, 0:samples] + c_ref[k, 0][None] * e
        e_all[k + 1] = e
    e_mine = jnp.zeros_like(e)
    for k in range(count):
        e_mine = e_mine + sel_ref[k][None] * e_all[k]
    t = jnp.zeros_like(e)
    t_mine = sel_ref[count - 1][None] * t
    for k in range(count - 1, 0, -1):
        offset = msg_ref[k, samples : 2 * samples] + c_ref[k, 1][None] * e_all[k]
        t = offset + c_ref[k, 2][None] * t
        t_mine = t_mine + sel_ref[k - 1][None] * t
    for i in range(out_ref.shape[1]):
        out_ref[:, i] = back_ref[:, i] + e_mine * h_ref[i][None] + t_mine * gu_ref[i][None]


def per_device(
    prior_noise,
    kappa_sq,
    horiz_cond,
    vert_cond,
    line_lower,
    line_pivot,
    deflation,
    obs_value,
    obs_weight,
    obs_cell,
    obs_count,
):
    samples = prior_noise.shape[0]
    vectors = deflation.shape[0]
    block_shape = prior_noise.shape[1:]
    layers = block_shape[0]
    cell_count = kappa_sq.size
    f32 = jnp.float32
    field = jax.ShapeDtypeStruct(block_shape, f32)
    gain_down, gain_up, h_field, consts = pl.pallas_call(
        prep_kernel,
        out_shape=(field, field, field, jax.ShapeDtypeStruct((3,) + block_shape[1:], f32)),
    )(line_lower, line_pivot)
    count = lax.axis_size("depth")
    value_rows = jnp.transpose(obs_value[:, 0, 0], (1, 0, 2)).reshape(count, -1)
    obs_rows = jnp.concatenate([value_rows, obs_weight[0, 0]], 1)
    lane = consts.shape[-1]
    obs_width = obs_rows.shape[1]
    obs_rows = jnp.pad(obs_rows, ((0, 0), (0, -obs_width % lane))).reshape(count, -1, lane)
    const_rows = jnp.broadcast_to(
        consts.reshape(1, -1, lane), (count, consts.size // lane, lane)
    )
    got = lax.all_to_all(
        jnp.concatenate([const_rows, obs_rows], 1), "depth", 0, 0, tiled=False
    )
    consts_all = got[:, : consts.size // lane].reshape((count,) + consts.shape)
    obs_got = got[:, consts.size // lane :].reshape(count, -1)[:, :obs_width]
    slots = obs_width // (samples + 1)
    got_value = jnp.transpose(obs_got[:, : samples * slots].reshape(count, samples, slots), (1, 0, 2))
    got_weight = obs_got[:, samples * slots :]
    slot_index = lax.broadcasted_iota(jnp.int32, obs_cell.shape[2:], 1)
    live_slot = (slot_index < obs_count[0, 0][:, None]).astype(f32).reshape(-1)
    weights = got_weight.reshape(-1) * live_slot
    targets = obs_cell.reshape(-1)
    planes, cols = cell_count // block_shape[2], block_shape[2]
    plane_hot = (
        lax.broadcasted_iota(jnp.int32, (planes, targets.size), 0) == (targets // cols)[None]
    ).astype(f32)
    col_hot = (
        lax.broadcasted_iota(jnp.int32, (targets.size, cols), 1) == (targets % cols)[:, None]
    ).astype(f32)
    slot_terms = jnp.concatenate([got_value.reshape(samples, -1) * weights[None], weights[None]], 0)
    placed = jnp.einsum(
        "po,joc->jpc", plane_hot, slot_terms[:, :, None] * col_hot[None], precision=PRECISE
    )
    obs_rhs = placed[:samples].reshape(prior_noise.shape)
    obs_diag = placed[samples].reshape(block_shape)

    joint = jnp.concatenate(
        [prior_noise, deflation, horiz_cond[None], vert_cond[None]], 0
    )
    j_below, j_above = neighbours(joint, "depth", 1)
    j_rowm, j_rowp = neighbours(joint, "tile", 2)
    lead = samples + vectors
    v_below, v_above = j_below[lead + 1], j_above[lead + 1]
    h_rowm, h_rowp = j_rowm[lead], j_rowp[lead]
    h_colp, h_colm = column_up(horiz_cond), column_down(horiz_cond)
    diag_part = (
        kappa_sq
        + horiz_cond * (h_rowp + h_rowm + h_colp + h_colm)
        + vert_cond * (v_above + v_below)
    )
    c_below, c_above = vert_cond * v_below, vert_cond * v_above
    c_rowm, c_rowp = horiz_cond * h_rowm, horiz_cond * h_rowp
    c_colm, c_colp = horiz_cond * h_colm, horiz_cond * h_colp

    def kcombine(u, below, above, rowm, rowp):
        flux = (
            c_rowp * rowp
            + c_rowm * rowm
            + c_colp * column_up(u)
            + c_colm * column_down(u)
            + c_above * above
            + c_below * below
        )
        return diag_part * u - flux

    def kapply(u):
        below, above = neighbours(u, "depth", 1)
        rowm, rowp = neighbours(u, "tile", 2)
        return kcombine(u, below, above, rowm, rowp)

    width = 2 * samples

    def line_solve(resid_in):
        back, message = pl.pallas_call(
            sweep_kernel,
            out_shape=(
                jax.ShapeDtypeStruct(resid_in.shape, f32),
                jax.ShapeDtypeStruct((2, samples) + block_shape[1:], f32),
            ),
        )(resid_in, line_lower, line_pivot)
        messages = gather_depth(message.reshape((width,) + block_shape[1:]))
        count = messages.shape[0]
        mine = lax.axis_index("depth")
        select = jnp.broadcast_to(
            (lax.iota(jnp.int32, count) == mine).astype(f32)[:, None, None],
            (count,) + block_shape[1:],
        )
        result = pl.pallas_call(
            scan_kernel,
            out_shape=jax.ShapeDtypeStruct(resid_in.shape, f32),
            scratch_shapes=[pltpu.VMEM((count, samples) + block_shape[1:], f32)],
        )(messages, consts_all, select, back, h_field, gain_up)
        return result

    k_joint = kcombine(
        joint[:lead], j_below[:lead], j_above[:lead], j_rowm[:lead], j_rowp[:lead]
    )
    right_side = k_joint[:samples] + obs_rhs
    basis_flat = deflation.reshape(vectors, cell_count)
    kbasis = k_joint[samples:]
    abasis_flat = (kapply(kbasis) + obs_diag * deflation).reshape(vectors, cell_count)
    gram_part = cells_dot(basis_flat, abasis_flat)
    proj_part = cells_dot(basis_flat, right_side.reshape(samples, cell_count))
    first = all_sum(jnp.concatenate([gram_part.reshape(-1), proj_part.reshape(-1)]))
    gram_total = first[: vectors * vectors].reshape(vectors, vectors)
    proj_rhs = first[vectors * vectors :].reshape(vectors, samples)
    gram_matrix = 0.5 * (gram_total + gram_total.T)
    chol_factor = jnp.linalg.cholesky(gram_matrix)

    def coarse(terms):
        return jax.scipy.linalg.cho_solve((chol_factor, True), terms)

    def expand(rows_flat, coarse_coef):
        return jnp.dot(coarse_coef.T, rows_flat, precision=PRECISE).reshape(prior_noise.shape)

    def inner_sum(left_side, right_part):
        return jnp.sum(left_side * right_part, axis=(1, 2, 3))

    def project(field_in):
        return cells_dot(abasis_flat, field_in.reshape(samples, cell_count))

    coarse_coef = coarse(proj_rhs)
    solution = expand(basis_flat, coarse_coef)
    residual = right_side - expand(abasis_flat, coarse_coef)

    precond = line_solve(residual)
    k_precond = kapply(precond)
    sums = all_sum(
        jnp.concatenate(
            [
                inner_sum(residual, precond),
                inner_sum(k_precond, k_precond) + inner_sum(obs_diag * precond, precond),
                project(precond).reshape(-1),
            ]
        )
    )
    rz_now, pap = sums[:samples], sums[samples : 2 * samples]
    proj_now = sums[2 * samples :].reshape(vectors, samples)
    a_precond = kapply(k_precond) + obs_diag * precond
    coarse_dir = coarse(proj_now)
    direction = precond - expand(basis_flat, coarse_dir)
    image_dir = a_precond - expand(abasis_flat, coarse_dir)
    curve_val = pap - jnp.sum(coarse_dir * proj_now, 0)
    step_field = (rz_now / curve_val)[:, None, None, None]
    solution = solution + step_field * direction
    residual = residual - step_field * image_dir

    precond = line_solve(residual)
    k_precond = kapply(precond)
    sums = all_sum(
        jnp.concatenate(
            [
                inner_sum(residual, precond),
                inner_sum(k_precond, k_precond) + inner_sum(obs_diag * precond, precond),
                inner_sum(image_dir, precond),
                project(precond).reshape(-1),
                project(direction).reshape(-1),
            ]
        )
    )
    rz_next, pap, cross = sums[:samples], sums[samples : 2 * samples], sums[2 * samples : 3 * samples]
    rest = sums[3 * samples :]
    proj_now = rest[: vectors * samples].reshape(vectors, samples)
    proj_old = rest[vectors * samples :].reshape(vectors, samples)
    a_precond = kapply(k_precond) + obs_diag * precond
    coarse_dir = coarse(proj_now)
    beta = rz_next / rz_now
    beta_ratio = beta[:, None, None, None]
    direction = precond + beta_ratio * direction - expand(basis_flat, coarse_dir)
    image_dir = a_precond + beta_ratio * image_dir - expand(abasis_flat, coarse_dir)
    curve_val = (
        pap
        + 2.0 * beta * cross
        + beta * beta * curve_val
        - jnp.sum(coarse_dir * proj_now, 0)
        - 2.0 * beta * jnp.sum(coarse_dir * proj_old, 0)
    )
    step_field = (rz_next / curve_val)[:, None, None, None]
    solution = solution + step_field * direction
    residual = residual - step_field * image_dir
    return (solution, residual)


def solution(mesh):
    return jax.shard_map(
        per_device,
        mesh=mesh,
        in_specs=(
            P(None, "depth", "tile", None),
            P("depth", "tile", None),
            P("depth", "tile", None),
            P("depth", "tile", None),
            P("depth", "tile", None),
            P("depth", "tile", None),
            P(None, "depth", "tile", None),
            P(None, "tile", "depth", None, None),
            P("tile", "depth", None, None),
            P("tile", "depth", None, None),
            P("tile", "depth", None),
        ),
        out_specs=(P(None, "depth", "tile", None), P(None, "depth", "tile", None)),
        check_vma=False,
    )
```
